512 devices in a mesh: patch: 128 (over y, z_lo, x), chan: 4 (over z_hi, core).
Axes of the slice: x: 4, y: 8, z: 8 (z_hi: 2, z_lo: 4; z = z_hi * 4 + z_lo), core: 2. Of those that a mesh axis runs over, the one named last changes fastest.
Arguments:
- latent: bfloat16 [8192, 1280], P('patch', 'chan'), may hold values from -6 to 6
- timestep: int32 [1], replicated, may hold values from 0 to 999
- norm_gain: float32 [1280], P('chan'), may hold values from 0.25 to 1.75
- norm_bias: float32 [1280], P('chan'), may hold values from -3 to 3
- w_time: bfloat16 [320, 1280], P(None, 'chan'), may hold values from -0.3125 to 0.3125
- w_query: bfloat16 [1280, 1024], P(None, 'chan'), may hold values from -0.15625 to 0.15625
- w_key: bfloat16 [1280, 1024], P(None, 'chan'), may hold values from -0.3125 to 0.3125
- w_value: bfloat16 [1280, 1024], P(None, 'chan'), may hold values from -0.15625 to 0.15625
- w_out: bfloat16 [1024, 1280], P('chan'), may hold values from -0.1875 to 0.1875
- stale_keys: bfloat16 [8192, 1024], P('patch', 'chan'), may hold values from -12 to 12
- stale_values: bfloat16 [8192, 1024], P('patch', 'chan'), may hold values from -6 to 6
Outputs:
- mixed: bfloat16 [8192, 1280], P('patch', 'chan')
- fresh_keys: bfloat16 [8192, 1024], P('patch', 'chan')
- fresh_values: bfloat16 [8192, 1024], P('patch', 'chan')
The draws below stay inside these ranges and needn't reach their ends.
All inputs are finite; a program needn't handle non-finite values.
Results may differ from the reference program's by a relative error of at most 0.006.
Values may be sent and summed in bfloat16 or wider, within the bound.
No kernel may reach another device: no remote copies, remote signals or barrier semaphores. Data moves between devices by JAX's collectives and lax.ppermute only.
A program may use at most 64 MiB of HBM per device.

```python
import math
import jax
import jax.numpy as jnp
from jax import lax

D = 1280
HEADS = 16
HEAD_DIM = 64
GROUPS = 32
TIME_DIM = 320
TOK_DEV = 64
TOKENS = 8192


def draw_stale_keys(key, part):
    entries = jax.random.normal(key, (TOKENS, HEADS * HEAD_DIM), jnp.float32) * 2.5
    entries = jnp.clip(entries, -12.0, 12.0)
    return entries.astype(jnp.bfloat16)


def block_scale(key, shape, cuts, smallest, high):
    def one(position, shards_of):
        steps = jax.random.uniform(jax.random.fold_in(jax.random.fold_in(key, 6), position), (shards_of,), jnp.float32, smallest / len(cuts), high / len(cuts))
        return jnp.repeat(jnp.exp(steps), shape[position] // shards_of).reshape((-1,) + (1,) * (len(shape) - position - 1))

    gain = one(*cuts[0])
    for cut in cuts[1:]:
        gain = gain * one(*cut)
    return gain


def centred(key, extent, scale, bound, shards=(), kind=jnp.bfloat16):
    array = jax.random.normal(key, extent, jnp.float32) * scale
    if len(shards) > 0:
        array = block_scale(key, extent, shards, -0.22, 0.18) * array
    return jnp.clip(array, min=-bound, max=bound).astype(kind)


def setup_inputs(seed: int = 0) -> dict:
    seeds = jax.random.split(jax.random.key(seed), 12)
    latent = centred(seeds[0], (TOKENS, D), 1.0, 6.0, ((0, 128), (1, 4)))
    timestep = jax.random.randint(seeds[1], (1,), 0, 1000).astype(jnp.int32)
    norm_gain = jnp.clip(1.0 + 0.15 * jax.random.normal(seeds[2], (D,), jnp.float32), 0.25, 1.75)
    norm_bias = centred(seeds[3], (D,), 0.5, 3.0, ((0, 4),), jnp.float32)
    w_time = centred(seeds[4], (TIME_DIM, D), TIME_DIM ** -0.5, 0.3125, ((1, 4),))
    w_query = centred(seeds[5], (D, HEADS * HEAD_DIM), D ** -0.5, 0.15625, ((1, 4),))
    w_key = centred(seeds[6], (D, HEADS * HEAD_DIM), (D // 4) ** -0.5, 0.3125, ((1, 4),))
    w_value = centred(seeds[7], (D, HEADS * HEAD_DIM), D ** -0.5, 0.15625, ((1, 4),))
    w_out = centred(seeds[8], (HEADS * HEAD_DIM, D), (HEADS * HEAD_DIM) ** -0.5, 0.1875, ((0, 4),))
    stale_keys = draw_stale_keys(jax.random.fold_in(seeds[11], 71), 0)
    stale_values = centred(seeds[10], (TOKENS, HEADS * HEAD_DIM), 1.0, 6.0, ((0, 128), (1, 4)))
    return dict(latent=latent, timestep=timestep, norm_gain=norm_gain, norm_bias=norm_bias, w_time=w_time, w_query=w_query, w_key=w_key, w_value=w_value, w_out=w_out, stale_keys=stale_keys, stale_values=stale_values)


def timestep_shift(timestep, w_time):
    half_dim = TIME_DIM // 2
    frequency = jnp.exp(-math.log(10000.0) * jnp.arange(half_dim, dtype=jnp.float32) / half_dim)
    angles = timestep[0].astype(jnp.float32) * frequency
    embedding = jnp.concatenate([jnp.cos(angles), jnp.sin(angles)])
    return jnp.dot(jax.nn.silu(embedding)[None, :], w_time.astype(jnp.float32), precision=lax.Precision.HIGHEST)[0]

def reference(latent, timestep, norm_gain, norm_bias, w_time, w_query, w_key, w_value, w_out, stale_keys, stale_values):
    width = D // GROUPS
    values = latent.astype(jnp.float32).reshape(TOKENS, GROUPS, width)
    group_mean = lax.optimization_barrier(jnp.mean(values, axis=(0, 2)))
    centered = values - group_mean[None, :, None]
    group_var = lax.optimization_barrier(jnp.mean(centered * centered, axis=(0, 2)))
    scaled = (centered * lax.rsqrt(group_var + 1e-05)[None, :, None]).reshape(TOKENS, D)
    normed = (scaled * norm_gain + norm_bias + timestep_shift(timestep, w_time)).astype(jnp.bfloat16)
    queries = jnp.dot(normed, w_query, preferred_element_type=jnp.float32).astype(jnp.bfloat16)
    fresh_keys = jnp.dot(normed, w_key, preferred_element_type=jnp.float32).astype(jnp.bfloat16)
    fresh_values = jnp.dot(normed, w_value, preferred_element_type=jnp.float32).astype(jnp.bfloat16)
    slab_count = TOKENS // TOK_DEV
    shape4 = (slab_count, TOK_DEV, HEADS, HEAD_DIM)
    query_slabs = queries.reshape(shape4)
    stale_k = stale_keys.reshape(shape4)
    stale_v = stale_values.reshape(shape4)
    fresh_k = fresh_keys.reshape(shape4)
    fresh_v = fresh_values.reshape(shape4)
    score_scale = HEAD_DIM ** (-0.5)

    def per_slab(index):
        key_block = stale_k.at[index].set(fresh_k[index]).astype(jnp.float32)
        value_block = stale_v.at[index].set(fresh_v[index]).astype(jnp.float32)
        query_block = query_slabs[index].astype(jnp.float32)
        score = jnp.einsum('qhd,bkhd->hqbk', query_block, key_block) * score_scale
        slab_max = lax.optimization_barrier(jnp.max(score, axis=-1))
        weight = jnp.exp(score - slab_max[..., None]).astype(jnp.bfloat16).astype(jnp.float32)
        slab_num = jnp.einsum('hqbk,bkhd->hqbd', weight, value_block)
        slab_den = lax.optimization_barrier(jnp.sum(weight, axis=-1))
        top = lax.optimization_barrier(jnp.max(slab_max, axis=-1))
        factor = jnp.exp(slab_max - top[..., None])
        numer = lax.optimization_barrier(jnp.sum(factor[..., None] * slab_num, axis=2))
        denom = lax.optimization_barrier(jnp.sum(factor * slab_den, axis=2))
        result = numer / denom[..., None]
        return jnp.transpose(result, (1, 0, 2)).reshape(TOK_DEV, HEADS * HEAD_DIM).astype(jnp.bfloat16)
    attended = lax.map(per_slab, jnp.arange(slab_count, dtype=jnp.int32)).reshape(TOKENS, HEADS * HEAD_DIM)
    projected = jnp.dot(attended, w_out, preferred_element_type=jnp.float32)
    mixed = (latent.astype(jnp.float32) + projected).astype(jnp.bfloat16)
    return (mixed, fresh_keys, fresh_values)
```

```python
import math

import jax
import jax.numpy as jnp
from jax import lax
from jax.sharding import Mesh
from jax.sharding import PartitionSpec as P

D = 1280
HEAD_DIM = 64
GROUPS = 32
PATCH_AXES = ("py", "pz", "px")
PATCH_SPLIT = (8, 4, 4)


def timestep_shift(timestep, w_time):
    half_dim = w_time.shape[0] // 2
    frequency = jnp.exp(-math.log(10000.0) * jnp.arange(half_dim, dtype=jnp.float32) / half_dim)
    angles = timestep[0].astype(jnp.float32) * frequency
    embedding = jnp.concatenate([jnp.cos(angles), jnp.sin(angles)])
    return jnp.dot(
        jax.nn.silu(embedding)[None, :], w_time.astype(jnp.float32), precision=lax.Precision.HIGHEST
    )[0]


def patch_sum(partial):
    for name in reversed(PATCH_AXES):
        partial = lax.optimization_barrier(lax.psum(partial, name))
    return partial


def local(
    latent,
    timestep,
    norm_gain,
    norm_bias,
    w_time,
    w_query,
    w_key,
    w_value,
    w_out,
    stale_keys,
    stale_values,
):
    rows_here, chan_width = latent.shape
    patch_count = math.prod(lax.axis_size(name) for name in PATCH_AXES)
    chan_count = lax.axis_size("chan")
    device = lax.axis_index(PATCH_AXES)
    local_groups = GROUPS // chan_count
    width = D // GROUPS
    values = latent.astype(jnp.float32).reshape(rows_here, local_groups, width)
    amount = rows_here * patch_count * width
    group_total = patch_sum(jnp.sum(values, axis=(0, 2)))
    group_mean = group_total / amount
    centered = values - group_mean[None, :, None]
    spread = patch_sum(jnp.sum(centered * centered, axis=(0, 2)))
    variance = spread / amount
    scaled = (centered * lax.rsqrt(variance + 1e-05)[None, :, None]).reshape(rows_here, chan_width)
    normed = (scaled * norm_gain + norm_bias + timestep_shift(timestep, w_time)).astype(
        jnp.bfloat16
    )
    inner = w_query.shape[1]
    shard_piece = lax.all_gather(normed, "chan", axis=1, tiled=True)
    outputs = []
    for index, weight_matrix in enumerate((w_query, w_key, w_value)):
        outputs.append(jnp.dot(shard_piece, weight_matrix, preferred_element_type=jnp.float32))
    summed = tuple(outputs)
    queries = summed[0].astype(jnp.bfloat16)
    fresh_keys = summed[1].astype(jnp.bfloat16)
    fresh_values = summed[2].astype(jnp.bfloat16)
    heads_here = inner // HEAD_DIM
    score_scale = HEAD_DIM ** (-0.5)
    query_heads = queries.reshape(rows_here, heads_here, HEAD_DIM)

    def slab_stats(key_block, value_block):
        score = (
            jnp.einsum("qhd,skhd->hqsk", query_heads, key_block, preferred_element_type=jnp.float32)
            * score_scale
        )
        block_max = jnp.max(score, axis=-1)
        weight = jnp.exp(score - block_max[..., None]).astype(jnp.bfloat16)
        block_num = jnp.einsum(
            "hqsk,skhd->hqsd", weight, value_block, preferred_element_type=jnp.float32
        )
        block_den = jnp.sum(weight.astype(jnp.float32), axis=-1)
        return (block_max, block_num, block_den)

    def combine(running, block_max, block_num, block_den):
        run_max, run_num, run_den = running
        new_max = jnp.maximum(run_max, jnp.max(block_max, axis=-1))
        keep_old = jnp.exp(run_max - new_max)
        factor = jnp.exp(block_max - new_max[..., None])
        run_num = keep_old[..., None] * run_num + jnp.sum(factor[..., None] * block_num, axis=2)
        run_den = keep_old * run_den + jnp.sum(factor * block_den, axis=2)
        return (new_max, run_num, run_den)

    home_max, home_num, home_den = slab_stats(
        fresh_keys.reshape(1, rows_here, heads_here, HEAD_DIM),
        fresh_values.reshape(1, rows_here, heads_here, HEAD_DIM),
    )
    start_state = (home_max[..., 0], home_num[:, :, 0], home_den[..., 0])
    stacked = jnp.stack([stale_keys, stale_values])
    for name in reversed(PATCH_AXES):
        stacked = lax.all_gather(stacked, name, axis=1, tiled=True)
    key_piece = stacked[0]
    value_piece = stacked[1]
    slab_count = key_piece.shape[0] // rows_here
    per_step = math.gcd(slab_count, 8)
    key_steps = key_piece.reshape(slab_count // per_step, per_step, rows_here, heads_here, HEAD_DIM)
    value_steps = value_piece.reshape(
        slab_count // per_step, per_step, rows_here, heads_here, HEAD_DIM
    )

    def advance(state, inputs):
        key_block, value_block, index = inputs
        block_max, block_num, block_den = slab_stats(key_block, value_block)
        slab_ids = index * per_step + jnp.arange(per_step, dtype=jnp.int32)
        is_home = slab_ids == device
        block_max = jnp.where(is_home[None, None, :], -1e30, block_max)
        return (combine(state, block_max, block_num, block_den), None)

    step_ids = jnp.arange(slab_count // per_step, dtype=jnp.int32)
    result, unused = lax.scan(advance, start_state, (key_steps, value_steps, step_ids))
    final_max, final_num, final_den = result
    attended = (
        jnp.transpose(final_num / final_den[..., None], (1, 0, 2))
        .reshape(rows_here, inner)
        .astype(jnp.bfloat16)
    )
    projected = lax.psum_scatter(
        jnp.dot(attended, w_out, preferred_element_type=jnp.float32).T,
        "chan",
        scatter_dimension=0,
        tiled=True,
    ).T
    mixed = (latent.astype(jnp.float32) + projected).astype(jnp.bfloat16)
    return (mixed, fresh_keys, fresh_values)


def solution(mesh):
    devices = mesh.devices.reshape(PATCH_SPLIT + (mesh.shape["chan"],))
    split_mesh = Mesh(devices, PATCH_AXES + ("chan",))
    rows = PATCH_AXES
    in_specs = (
        P(rows, "chan"),
        P(),
        P("chan"),
        P("chan"),
        P(None, "chan"),
        P(None, "chan"),
        P(None, "chan"),
        P(None, "chan"),
        P("chan", None),
        P(rows, "chan"),
        P(rows, "chan"),
    )
    out_specs = (P(rows, "chan"), P(rows, "chan"), P(rows, "chan"))
    return jax.shard_map(
        local, mesh=split_mesh, in_specs=in_specs, out_specs=out_specs, check_vma=False
    )
```

```python
import math

import jax
import jax.numpy as jnp
from jax import lax
from jax.sharding import Mesh
from jax.sharding import PartitionSpec as P

D = 1280
HEAD_DIM = 64
GROUPS = 32
PATCH_AXES = ("py", "pz", "px")
PATCH_SPLIT = (8, 4, 4)


def timestep_shift(timestep, w_time):
    half_dim = w_time.shape[0] // 2
    frequency = jnp.exp(-math.log(10000.0) * jnp.arange(half_dim, dtype=jnp.float32) / half_dim)
    angles = timestep[0].astype(jnp.float32) * frequency
    embedding = jnp.concatenate([jnp.cos(angles), jnp.sin(angles)])
    return jnp.dot(
        jax.nn.silu(embedding)[None, :], w_time.astype(jnp.float32), precision=lax.Precision.HIGHEST
    )[0]


def patch_sum(partial):
    for name in reversed(PATCH_AXES):
        partial = lax.optimization_barrier(lax.psum(partial, name))
    return partial


def local(
    latent,
    timestep,
    norm_gain,
    norm_bias,
    w_time,
    w_query,
    w_key,
    w_value,
    w_out,
    stale_keys,
    stale_values,
):
    rows_here, chan_width = latent.shape
    patch_count = math.prod(lax.axis_size(name) for name in PATCH_AXES)
    chan_count = lax.axis_size("chan")
    device = lax.axis_index(PATCH_AXES)
    local_groups = GROUPS // chan_count
    width = D // GROUPS
    values = latent.astype(jnp.float32).reshape(rows_here, local_groups, width)
    amount = rows_here * patch_count * width
    group_total = patch_sum(jnp.sum(values, axis=(0, 2)))
    group_mean = group_total / amount
    centered = values - group_mean[None, :, None]
    spread = patch_sum(jnp.sum(centered * centered, axis=(0, 2)))
    variance = spread / amount
    scaled = (centered * lax.rsqrt(variance + 1e-05)[None, :, None]).reshape(rows_here, chan_width)
    normed = (scaled * norm_gain + norm_bias + timestep_shift(timestep, w_time)).astype(
        jnp.bfloat16
    )
    inner = w_query.shape[1]
    shard_piece = lax.all_gather(normed, "chan", axis=1, tiled=True)
    outputs = []
    for index, weight_matrix in enumerate((w_query, w_key, w_value)):
        outputs.append(jnp.dot(shard_piece, weight_matrix, preferred_element_type=jnp.float32))
    summed = tuple(outputs)
    queries = summed[0].astype(jnp.bfloat16)
    fresh_keys = summed[1].astype(jnp.bfloat16)
    fresh_values = summed[2].astype(jnp.bfloat16)
    heads_here = inner // HEAD_DIM
    score_scale = HEAD_DIM ** (-0.5)
    split = lax.axis_size("px")
    own_head = lax.axis_index("px")

    stacked = lax.all_gather(jnp.stack([stale_keys, stale_values]), "px", axis=1, tiled=True)
    stacked = lax.dynamic_slice_in_dim(stacked, own_head * HEAD_DIM, HEAD_DIM, axis=2)
    for name in reversed(PATCH_AXES[:-1]):
        stacked = lax.all_gather(stacked, name, axis=1, tiled=True)
    slab_count = stacked.shape[1] // rows_here
    stale_k = stacked[0].reshape(slab_count, rows_here, HEAD_DIM)
    stale_v = stacked[1].reshape(slab_count, rows_here, HEAD_DIM)

    fresh = jnp.stack([queries, fresh_keys, fresh_values]).reshape(
        3, rows_here, heads_here, HEAD_DIM
    )
    fresh = lax.all_to_all(fresh, "px", 2, 1, tiled=True).reshape(3, split, rows_here, HEAD_DIM)
    query_rows = fresh[0].reshape(split * rows_here, HEAD_DIM)

    score = (
        jnp.einsum("qd,skd->qsk", query_rows, stale_k, preferred_element_type=jnp.float32)
        * score_scale
    )
    block_max = jnp.max(score, axis=-1)
    weight = jnp.exp(score - block_max[..., None]).astype(jnp.bfloat16)
    block_num = jnp.einsum("qsk,skd->qsd", weight, stale_v, preferred_element_type=jnp.float32)
    block_den = jnp.sum(weight.astype(jnp.float32), axis=-1)

    home_score = (
        jnp.einsum("gqd,gkd->gqk", fresh[0], fresh[1], preferred_element_type=jnp.float32)
        * score_scale
    )
    home_max = jnp.max(home_score, axis=-1)
    home_weight = jnp.exp(home_score - home_max[..., None]).astype(jnp.bfloat16)
    home_num = jnp.einsum("gqk,gkd->gqd", home_weight, fresh[2], preferred_element_type=jnp.float32)
    home_den = jnp.sum(home_weight.astype(jnp.float32), axis=-1)
    home_max = home_max.reshape(split * rows_here, 1)
    home_num = home_num.reshape(split * rows_here, 1, HEAD_DIM)
    home_den = home_den.reshape(split * rows_here, 1)

    first_slab = (device // split) * split
    query_slab = first_slab + jnp.arange(split * rows_here, dtype=jnp.int32) // rows_here
    is_home = query_slab[:, None] == jnp.arange(slab_count, dtype=jnp.int32)[None, :]
    block_max = jnp.where(is_home, home_max, block_max)
    block_den = jnp.where(is_home, home_den, block_den)
    block_num = jnp.where(is_home[..., None], home_num, block_num)

    top = jnp.max(block_max, axis=-1)
    factor = jnp.exp(block_max - top[:, None])
    numer = jnp.sum(factor[..., None] * block_num, axis=1)
    denom = jnp.sum(factor * block_den, axis=1)
    result = (numer / denom[:, None]).astype(jnp.bfloat16)
    result = result.reshape(split, rows_here, 1, HEAD_DIM)
    attended = lax.all_to_all(result, "px", 0, 2, tiled=True).reshape(rows_here, inner)
    projected = lax.psum_scatter(
        jnp.dot(attended, w_out, preferred_element_type=jnp.float32).T,
        "chan",
        scatter_dimension=0,
        tiled=True,
    ).T
    mixed = (latent.astype(jnp.float32) + projected).astype(jnp.bfloat16)
    return (mixed, fresh_keys, fresh_values)


def solution(mesh):
    devices = mesh.devices.reshape(PATCH_SPLIT + (mesh.shape["chan"],))
    split_mesh = Mesh(devices, PATCH_AXES + ("chan",))
    rows = PATCH_AXES
    in_specs = (
        P(rows, "chan"),
        P(),
        P("chan"),
        P("chan"),
        P(None, "chan"),
        P(None, "chan"),
        P(None, "chan"),
        P(None, "chan"),
        P("chan", None),
        P(rows, "chan"),
        P(rows, "chan"),
    )
    out_specs = (P(rows, "chan"), P(rows, "chan"), P(rows, "chan"))
    return jax.shard_map(
        local, mesh=split_mesh, in_specs=in_specs, out_specs=out_specs, check_vma=False
    )
```

```python
import math

import jax
import jax.numpy as jnp
from jax import lax
from jax.sharding import Mesh
from jax.sharding import PartitionSpec as P

D = 1280
HEAD_DIM = 64
GROUPS = 32
PATCH_AXES = ("py", "pz", "px")
PATCH_SPLIT = (8, 4, 4)


def timestep_shift(timestep, w_time):
    half_dim = w_time.shape[0] // 2
    frequency = jnp.exp(-math.log(10000.0) * jnp.arange(half_dim, dtype=jnp.float32) / half_dim)
    angles = timestep[0].astype(jnp.float32) * frequency
    embedding = jnp.concatenate([jnp.cos(angles), jnp.sin(angles)])
    return jnp.dot(
        jax.nn.silu(embedding)[None, :], w_time.astype(jnp.float32), precision=lax.Precision.HIGHEST
    )[0]


def patch_sum(partial):
    for name in reversed(PATCH_AXES):
        partial = lax.optimization_barrier(lax.psum(partial, name))
    return partial


def local(
    latent,
    timestep,
    norm_gain,
    norm_bias,
    w_time,
    w_query,
    w_key,
    w_value,
    w_out,
    stale_keys,
    stale_values,
):
    rows_here, chan_width = latent.shape
    patch_count = math.prod(lax.axis_size(name) for name in PATCH_AXES)
    chan_count = lax.axis_size("chan")
    device = lax.axis_index(PATCH_AXES)
    local_groups = GROUPS // chan_count
    width = D // GROUPS
    values = latent.astype(jnp.float32).reshape(rows_here, local_groups, width)
    here = rows_here * width
    local_mean = jnp.sum(values, axis=(0, 2)) / here
    local_spread = jnp.sum(jnp.square(values - local_mean[None, :, None]), axis=(0, 2))
    gathered = jnp.stack([local_mean, local_spread])[None]
    for name in reversed(PATCH_AXES):
        gathered = lax.all_gather(gathered, name, axis=0, tiled=True)
    group_mean = jnp.mean(gathered[:, 0], axis=0)
    offset = gathered[:, 0] - group_mean[None, :]
    spread = jnp.sum(gathered[:, 1], axis=0) + here * jnp.sum(offset * offset, axis=0)
    variance = spread / (here * patch_count)
    centered = values - group_mean[None, :, None]
    scaled = (centered * lax.rsqrt(variance + 1e-05)[None, :, None]).reshape(rows_here, chan_width)
    normed = (scaled * norm_gain + norm_bias + timestep_shift(timestep, w_time)).astype(
        jnp.bfloat16
    )
    inner = w_query.shape[1]
    shard_piece = lax.all_gather(normed, "chan", axis=1, tiled=True)
    outputs = []
    for index, weight_matrix in enumerate((w_query, w_key, w_value)):
        outputs.append(jnp.dot(shard_piece, weight_matrix, preferred_element_type=jnp.float32))
    summed = tuple(outputs)
    queries = summed[0].astype(jnp.bfloat16)
    fresh_keys = summed[1].astype(jnp.bfloat16)
    fresh_values = summed[2].astype(jnp.bfloat16)
    heads_here = inner // HEAD_DIM
    score_scale = HEAD_DIM ** (-0.5)
    split = lax.axis_size("px")
    own_head = lax.axis_index("px")

    stacked = lax.all_gather(jnp.stack([stale_keys, stale_values]), "px", axis=1, tiled=True)
    stacked = lax.dynamic_slice_in_dim(stacked, own_head * HEAD_DIM, HEAD_DIM, axis=2)
    for name in PATCH_AXES[:-1]:
        stacked = lax.all_gather(stacked, name, axis=1, tiled=True)
    slab_count = stacked.shape[1] // rows_here
    stale_k = stacked[0].reshape(slab_count, rows_here, HEAD_DIM)
    stale_v = stacked[1].reshape(slab_count, rows_here, HEAD_DIM)

    fresh = jnp.stack([queries, fresh_keys, fresh_values]).reshape(
        3, rows_here, heads_here, HEAD_DIM
    )
    fresh = lax.all_to_all(fresh, "px", 2, 1, tiled=True).reshape(3, split, rows_here, HEAD_DIM)
    query_rows = fresh[0].reshape(split * rows_here, HEAD_DIM)

    score = (
        jnp.einsum("qd,skd->qsk", query_rows, stale_k, preferred_element_type=jnp.float32)
        * score_scale
    )
    block_max = jnp.max(score, axis=-1)
    weight = jnp.exp(score - block_max[..., None]).astype(jnp.bfloat16)
    block_num = jnp.einsum("qsk,skd->qsd", weight, stale_v, preferred_element_type=jnp.float32)
    block_den = jnp.sum(weight.astype(jnp.float32), axis=-1)

    home_score = (
        jnp.einsum("gqd,gkd->gqk", fresh[0], fresh[1], preferred_element_type=jnp.float32)
        * score_scale
    )
    home_max = jnp.max(home_score, axis=-1)
    home_weight = jnp.exp(home_score - home_max[..., None]).astype(jnp.bfloat16)
    home_num = jnp.einsum("gqk,gkd->gqd", home_weight, fresh[2], preferred_element_type=jnp.float32)
    home_den = jnp.sum(home_weight.astype(jnp.float32), axis=-1)
    home_max = home_max.reshape(split * rows_here, 1)
    home_num = home_num.reshape(split * rows_here, 1, HEAD_DIM)
    home_den = home_den.reshape(split * rows_here, 1)

    first_slab = (lax.axis_index("pz") * lax.axis_size("py") + lax.axis_index("py")) * split
    query_slab = first_slab + jnp.arange(split * rows_here, dtype=jnp.int32) // rows_here
    is_home = query_slab[:, None] == jnp.arange(slab_count, dtype=jnp.int32)[None, :]
    block_max = jnp.where(is_home, home_max, block_max)
    block_den = jnp.where(is_home, home_den, block_den)
    block_num = jnp.where(is_home[..., None], home_num, block_num)

    top = jnp.max(block_max, axis=-1)
    factor = jnp.exp(block_max - top[:, None])
    numer = jnp.sum(factor[..., None] * block_num, axis=1)
    denom = jnp.sum(factor * block_den, axis=1)
    result = (numer / denom[:, None]).astype(jnp.bfloat16)
    result = result.reshape(split, rows_here, 1, HEAD_DIM)
    attended = lax.all_to_all(result, "px", 0, 2, tiled=True).reshape(rows_here, inner)
    attended = lax.all_gather(attended, "chan", axis=1, tiled=True)
    out_columns = lax.all_to_all(w_out, "chan", 1, 0, tiled=True)
    projected = jnp.dot(attended, out_columns, preferred_element_type=jnp.float32)
    mixed = (latent.astype(jnp.float32) + projected).astype(jnp.bfloat16)
    return (mixed, fresh_keys, fresh_values)


def solution(mesh):
    devices = mesh.devices.reshape(PATCH_SPLIT + (mesh.shape["chan"],))
    split_mesh = Mesh(devices, PATCH_AXES + ("chan",))
    rows = PATCH_AXES
    in_specs = (
        P(rows, "chan"),
        P(),
        P("chan"),
        P("chan"),
        P(None, "chan"),
        P(None, "chan"),
        P(None, "chan"),
        P(None, "chan"),
        P("chan", None),
        P(rows, "chan"),
        P(rows, "chan"),
    )
    out_specs = (P(rows, "chan"), P(rows, "chan"), P(rows, "chan"))
    return jax.shard_map(
        local, mesh=split_mesh, in_specs=in_specs, out_specs=out_specs, check_vma=False
    )
```

```python
import math

import jax
import jax.numpy as jnp
from jax import lax
from jax.sharding import Mesh
from jax.sharding import PartitionSpec as P

D = 1280
HEAD_DIM = 64
GROUPS = 32
PATCH_AXES = ("py", "pz", "px")
PATCH_SPLIT = (8, 4, 4)


def timestep_shift(timestep, w_time):
    half_dim = w_time.shape[0] // 2
    frequency = jnp.exp(-math.log(10000.0) * jnp.arange(half_dim, dtype=jnp.float32) / half_dim)
    angles = timestep[0].astype(jnp.float32) * frequency
    embedding = jnp.concatenate([jnp.cos(angles), jnp.sin(angles)])
    return jnp.dot(
        jax.nn.silu(embedding)[None, :], w_time.astype(jnp.float32), precision=lax.Precision.HIGHEST
    )[0]


def patch_sum(partial):
    for name in reversed(PATCH_AXES):
        partial = lax.optimization_barrier(lax.psum(partial, name))
    return partial


def local(
    latent,
    timestep,
    norm_gain,
    norm_bias,
    w_time,
    w_query,
    w_key,
    w_value,
    w_out,
    stale_keys,
    stale_values,
):
    rows_here, chan_width = latent.shape
    patch_count = math.prod(lax.axis_size(name) for name in PATCH_AXES)
    chan_count = lax.axis_size("chan")
    device = lax.axis_index(PATCH_AXES)
    local_groups = GROUPS // chan_count
    width = D // GROUPS
    values = latent.astype(jnp.float32).reshape(rows_here, local_groups, width)
    here = rows_here * width
    local_mean = jnp.sum(values, axis=(0, 2)) / here
    local_spread = jnp.sum(jnp.square(values - local_mean[None, :, None]), axis=(0, 2))
    gathered = jnp.stack([local_mean, local_spread])[None]
    for name in reversed(PATCH_AXES):
        gathered = lax.all_gather(gathered, name, axis=0, tiled=True)
    group_mean = jnp.mean(gathered[:, 0], axis=0)
    offset = gathered[:, 0] - group_mean[None, :]
    spread = jnp.sum(gathered[:, 1], axis=0) + here * jnp.sum(offset * offset, axis=0)
    variance = spread / (here * patch_count)
    centered = values - group_mean[None, :, None]
    scaled = (centered * lax.rsqrt(variance + 1e-05)[None, :, None]).reshape(rows_here, chan_width)
    normed = (scaled * norm_gain + norm_bias + timestep_shift(timestep, w_time)).astype(
        jnp.bfloat16
    )
    inner = w_query.shape[1]
    shard_piece = lax.all_gather(normed, "chan", axis=1, tiled=True)
    outputs = []
    for index, weight_matrix in enumerate((w_query, w_key, w_value)):
        outputs.append(jnp.dot(shard_piece, weight_matrix, preferred_element_type=jnp.float32))
    summed = tuple(outputs)
    queries = summed[0].astype(jnp.bfloat16)
    fresh_keys = summed[1].astype(jnp.bfloat16)
    fresh_values = summed[2].astype(jnp.bfloat16)
    heads_here = inner // HEAD_DIM
    score_scale = HEAD_DIM ** (-0.5)
    split = lax.axis_size("px")
    own_head = lax.axis_index("px")

    stacked = lax.all_gather(jnp.stack([stale_keys, stale_values]), "px", axis=1, tiled=True)
    stacked = lax.dynamic_slice_in_dim(stacked, own_head * HEAD_DIM, HEAD_DIM, axis=2)
    stacked = lax.all_gather(stacked, PATCH_AXES[:-1], axis=1, tiled=True)
    slab_count = stacked.shape[1] // rows_here
    stale_k = stacked[0].reshape(slab_count, rows_here, HEAD_DIM)
    stale_v = stacked[1].reshape(slab_count, rows_here, HEAD_DIM)

    fresh = jnp.stack([queries, fresh_keys, fresh_values]).reshape(
        3, rows_here, heads_here, HEAD_DIM
    )
    fresh = lax.all_to_all(fresh, "px", 2, 1, tiled=True).reshape(3, split, rows_here, HEAD_DIM)
    query_rows = fresh[0].reshape(split * rows_here, HEAD_DIM)

    score = (
        jnp.einsum("qd,skd->qsk", query_rows, stale_k, preferred_element_type=jnp.float32)
        * score_scale
    )
    block_max = jnp.max(score, axis=-1)
    weight = jnp.exp(score - block_max[..., None]).astype(jnp.bfloat16)
    block_num = jnp.einsum("qsk,skd->qsd", weight, stale_v, preferred_element_type=jnp.float32)
    block_den = jnp.sum(weight.astype(jnp.float32), axis=-1)

    home_score = (
        jnp.einsum("gqd,gkd->gqk", fresh[0], fresh[1], preferred_element_type=jnp.float32)
        * score_scale
    )
    home_max = jnp.max(home_score, axis=-1)
    home_weight = jnp.exp(home_score - home_max[..., None]).astype(jnp.bfloat16)
    home_num = jnp.einsum("gqk,gkd->gqd", home_weight, fresh[2], preferred_element_type=jnp.float32)
    home_den = jnp.sum(home_weight.astype(jnp.float32), axis=-1)
    home_max = home_max.reshape(split * rows_here, 1)
    home_num = home_num.reshape(split * rows_here, 1, HEAD_DIM)
    home_den = home_den.reshape(split * rows_here, 1)

    first_slab = (device // split) * split
    query_slab = first_slab + jnp.arange(split * rows_here, dtype=jnp.int32) // rows_here
    is_home = query_slab[:, None] == jnp.arange(slab_count, dtype=jnp.int32)[None, :]
    block_max = jnp.where(is_home, home_max, block_max)
    block_den = jnp.where(is_home, home_den, block_den)
    block_num = jnp.where(is_home[..., None], home_num, block_num)

    top = jnp.max(block_max, axis=-1)
    factor = jnp.exp(block_max - top[:, None])
    numer = jnp.sum(factor[..., None] * block_num, axis=1)
    denom = jnp.sum(factor * block_den, axis=1)
    result = (numer / denom[:, None]).astype(jnp.bfloat16)
    result = result.reshape(1, split, rows_here, HEAD_DIM)
    result = jnp.broadcast_to(result, (chan_count, split, rows_here, HEAD_DIM))
    result = result.reshape(chan_count * split, rows_here, HEAD_DIM)
    attended = lax.all_to_all(result, ("chan", "px"), 0, 0, tiled=True)
    attended = jnp.transpose(attended, (1, 0, 2)).reshape(rows_here, chan_count * inner)
    out_columns = lax.all_to_all(w_out, "chan", 1, 0, tiled=True)
    projected = jnp.dot(attended, out_columns, preferred_element_type=jnp.float32)
    mixed = (latent.astype(jnp.float32) + projected).astype(jnp.bfloat16)
    return (mixed, fresh_keys, fresh_values)


def solution(mesh):
    devices = mesh.devices.reshape(PATCH_SPLIT + (mesh.shape["chan"],))
    split_mesh = Mesh(devices, PATCH_AXES + ("chan",))
    rows = PATCH_AXES
    in_specs = (
        P(rows, "chan"),
        P(),
        P("chan"),
        P("chan"),
        P(None, "chan"),
        P(None, "chan"),
        P(None, "chan"),
        P(None, "chan"),
        P("chan", None),
        P(rows, "chan"),
        P(rows, "chan"),
    )
    out_specs = (P(rows, "chan"), P(rows, "chan"), P(rows, "chan"))
    return jax.shard_map(
        local, mesh=split_mesh, in_specs=in_specs, out_specs=out_specs, check_vma=False
    )
```

```python
import math

import jax
import jax.numpy as jnp
from jax import lax
from jax.sharding import Mesh
from jax.sharding import PartitionSpec as P

D = 1280
HEAD_DIM = 64
GROUPS = 32
PATCH_AXES = ("py", "pz", "px")
PATCH_SPLIT = (8, 4, 4)


def timestep_shift(timestep, w_time):
    half_dim = w_time.shape[0] // 2
    frequency = jnp.exp(-math.log(10000.0) * jnp.arange(half_dim, dtype=jnp.float32) / half_dim)
    angles = timestep[0].astype(jnp.float32) * frequency
    embedding = jnp.concatenate([jnp.cos(angles), jnp.sin(angles)])
    return jnp.dot(
        jax.nn.silu(embedding)[None, :], w_time.astype(jnp.float32), precision=lax.Precision.HIGHEST
    )[0]


def patch_sum(partial):
    for name in reversed(PATCH_AXES):
        partial = lax.optimization_barrier(lax.psum(partial, name))
    return partial


def local(
    latent,
    timestep,
    norm_gain,
    norm_bias,
    w_time,
    w_query,
    w_key,
    w_value,
    w_out,
    stale_keys,
    stale_values,
):
    rows_here, chan_width = latent.shape
    patch_count = math.prod(lax.axis_size(name) for name in PATCH_AXES)
    chan_count = lax.axis_size("chan")
    device = lax.axis_index(PATCH_AXES)
    local_groups = GROUPS // chan_count
    width = D // GROUPS
    values = latent.astype(jnp.float32).reshape(rows_here, local_groups, width)
    count = rows_here * width
    group_mean = jnp.sum(values, axis=(0, 2)) / count
    spread = jnp.sum(jnp.square(values - group_mean[None, :, None]), axis=(0, 2))
    for name in reversed(PATCH_AXES):
        gathered = lax.all_gather(jnp.stack([group_mean, spread]), name)
        group_mean = jnp.mean(gathered[:, 0], axis=0)
        offset = gathered[:, 0] - group_mean[None, :]
        spread = jnp.sum(gathered[:, 1], axis=0) + count * jnp.sum(offset * offset, axis=0)
        count = count * gathered.shape[0]
    variance = spread / count
    centered = values - group_mean[None, :, None]
    scaled = (centered * lax.rsqrt(variance + 1e-05)[None, :, None]).reshape(rows_here, chan_width)
    normed = (scaled * norm_gain + norm_bias + timestep_shift(timestep, w_time)).astype(
        jnp.bfloat16
    )
    inner = w_query.shape[1]
    shard_piece = lax.all_gather(normed, "chan", axis=1, tiled=True)
    outputs = []
    for index, weight_matrix in enumerate((w_query, w_key, w_value)):
        outputs.append(jnp.dot(shard_piece, weight_matrix, preferred_element_type=jnp.float32))
    summed = tuple(outputs)
    queries = summed[0].astype(jnp.bfloat16)
    fresh_keys = summed[1].astype(jnp.bfloat16)
    fresh_values = summed[2].astype(jnp.bfloat16)
    heads_here = inner // HEAD_DIM
    score_scale = HEAD_DIM ** (-0.5)
    split = lax.axis_size("px")
    own_head = lax.axis_index("px")

    stacked = lax.all_gather(jnp.stack([stale_keys, stale_values]), "px", axis=1, tiled=True)
    stacked = lax.dynamic_slice_in_dim(stacked, own_head * HEAD_DIM, HEAD_DIM, axis=2)
    for name in reversed(PATCH_AXES[:-1]):
        stacked = lax.all_gather(stacked, name, axis=1, tiled=True)
    slab_count = stacked.shape[1] // rows_here
    stale_k = stacked[0].reshape(slab_count, rows_here, HEAD_DIM)
    stale_v = stacked[1].reshape(slab_count, rows_here, HEAD_DIM)

    fresh = jnp.stack([queries, fresh_keys, fresh_values]).reshape(
        3, rows_here, heads_here, HEAD_DIM
    )
    fresh = lax.all_to_all(fresh, "px", 2, 1, tiled=True).reshape(3, split, rows_here, HEAD_DIM)
    query_rows = fresh[0].reshape(split * rows_here, HEAD_DIM)

    score = (
        jnp.einsum("qd,skd->qsk", query_rows, stale_k, preferred_element_type=jnp.float32)
        * score_scale
    )
    block_max = jnp.max(score, axis=-1)
    weight = jnp.exp(score - block_max[..., None]).astype(jnp.bfloat16)
    block_num = jnp.einsum("qsk,skd->qsd", weight, stale_v, preferred_element_type=jnp.float32)
    block_den = jnp.sum(weight.astype(jnp.float32), axis=-1)

    home_score = (
        jnp.einsum("gqd,gkd->gqk", fresh[0], fresh[1], preferred_element_type=jnp.float32)
        * score_scale
    )
    home_max = jnp.max(home_score, axis=-1)
    home_weight = jnp.exp(home_score - home_max[..., None]).astype(jnp.bfloat16)
    home_num = jnp.einsum("gqk,gkd->gqd", home_weight, fresh[2], preferred_element_type=jnp.float32)
    home_den = jnp.sum(home_weight.astype(jnp.float32), axis=-1)
    home_max = home_max.reshape(split * rows_here, 1)
    home_num = home_num.reshape(split * rows_here, 1, HEAD_DIM)
    home_den = home_den.reshape(split * rows_here, 1)

    first_slab = (device // split) * split
    query_slab = first_slab + jnp.arange(split * rows_here, dtype=jnp.int32) // rows_here
    is_home = query_slab[:, None] == jnp.arange(slab_count, dtype=jnp.int32)[None, :]
    block_max = jnp.where(is_home, home_max, block_max)
    block_den = jnp.where(is_home, home_den, block_den)
    block_num = jnp.where(is_home[..., None], home_num, block_num)

    top = jnp.max(block_max, axis=-1)
    factor = jnp.exp(block_max - top[:, None])
    numer = jnp.sum(factor[..., None] * block_num, axis=1)
    denom = jnp.sum(factor * block_den, axis=1)
    result = (numer / denom[:, None]).astype(jnp.bfloat16)
    result = result.reshape(1, split, rows_here, HEAD_DIM)
    result = jnp.broadcast_to(result, (chan_count, split, rows_here, HEAD_DIM))
    result = result.reshape(chan_count * split, rows_here, HEAD_DIM)
    attended = lax.all_to_all(result, ("chan", "px"), 0, 0, tiled=True)
    attended = jnp.transpose(attended, (1, 0, 2)).reshape(rows_here, chan_count * inner)
    out_columns = lax.all_to_all(w_out, "chan", 1, 0, tiled=True)
    projected = jnp.dot(attended, out_columns, preferred_element_type=jnp.float32)
    mixed = (latent.astype(jnp.float32) + projected).astype(jnp.bfloat16)
    return (mixed, fresh_keys, fresh_values)


def solution(mesh):
    devices = mesh.devices.reshape(PATCH_SPLIT + (mesh.shape["chan"],))
    split_mesh = Mesh(devices, PATCH_AXES + ("chan",))
    rows = PATCH_AXES
    in_specs = (
        P(rows, "chan"),
        P(),
        P("chan"),
        P("chan"),
        P(None, "chan"),
        P(None, "chan"),
        P(None, "chan"),
        P(None, "chan"),
        P("chan", None),
        P(rows, "chan"),
        P(rows, "chan"),
    )
    out_specs = (P(rows, "chan"), P(rows, "chan"), P(rows, "chan"))
    return jax.shard_map(
        local, mesh=split_mesh, in_specs=in_specs, out_specs=out_specs, check_vma=False
    )
```

```python
import math

import jax
import jax.numpy as jnp
from jax import lax
from jax.sharding import Mesh
from jax.sharding import PartitionSpec as P

D = 1280
HEAD_DIM = 64
GROUPS = 32
PATCH_AXES = ("py", "pz", "px")
PATCH_SPLIT = (8, 4, 4)


def timestep_shift(timestep, w_time):
    half_dim = w_time.shape[0] // 2
    frequency = jnp.exp(-math.log(10000.0) * jnp.arange(half_dim, dtype=jnp.float32) / half_dim)
    angles = timestep[0].astype(jnp.float32) * frequency
    embedding = jnp.concatenate([jnp.cos(angles), jnp.sin(angles)])
    return jnp.dot(
        jax.nn.silu(embedding)[None, :], w_time.astype(jnp.float32), precision=lax.Precision.HIGHEST
    )[0]


def patch_sum(partial):
    for name in reversed(PATCH_AXES):
        partial = lax.optimization_barrier(lax.psum(partial, name))
    return partial


def local(
    latent,
    timestep,
    norm_gain,
    norm_bias,
    w_time,
    w_query,
    w_key,
    w_value,
    w_out,
    stale_keys,
    stale_values,
):
    rows_here, chan_width = latent.shape
    patch_count = math.prod(lax.axis_size(name) for name in PATCH_AXES)
    chan_count = lax.axis_size("chan")
    device = lax.axis_index(PATCH_AXES)
    local_groups = GROUPS // chan_count
    width = D // GROUPS
    values = latent.astype(jnp.float32).reshape(rows_here, local_groups, width)
    count = rows_here * width
    group_mean = jnp.sum(values, axis=(0, 2)) / count
    spread = jnp.sum(jnp.square(values - group_mean[None, :, None]), axis=(0, 2))
    for name in reversed(PATCH_AXES):
        gathered = lax.all_gather(jnp.stack([group_mean, spread]), name)
        group_mean = jnp.mean(gathered[:, 0], axis=0)
        offset = gathered[:, 0] - group_mean[None, :]
        spread = jnp.sum(gathered[:, 1], axis=0) + count * jnp.sum(offset * offset, axis=0)
        count = count * gathered.shape[0]
    variance = spread / count
    centered = values - group_mean[None, :, None]
    scaled = (centered * lax.rsqrt(variance + 1e-05)[None, :, None]).reshape(rows_here, chan_width)
    normed = (scaled * norm_gain + norm_bias + timestep_shift(timestep, w_time)).astype(
        jnp.bfloat16
    )
    inner = w_query.shape[1]
    shard_piece = lax.all_gather(normed, "chan", axis=1, tiled=True)
    outputs = []
    for index, weight_matrix in enumerate((w_query, w_key, w_value)):
        outputs.append(jnp.dot(shard_piece, weight_matrix, preferred_element_type=jnp.float32))
    summed = tuple(outputs)
    queries = summed[0].astype(jnp.bfloat16)
    fresh_keys = summed[1].astype(jnp.bfloat16)
    fresh_values = summed[2].astype(jnp.bfloat16)
    heads_here = inner // HEAD_DIM
    score_scale = HEAD_DIM ** (-0.5)
    split = lax.axis_size("px")
    own_head = lax.axis_index("px")

    stacked = jnp.stack([stale_keys, stale_values]).reshape(2, rows_here, heads_here, HEAD_DIM)
    stacked = lax.all_to_all(stacked, "px", 2, 1, tiled=True).reshape(2, split * rows_here, HEAD_DIM)
    for name in reversed(PATCH_AXES[:-1]):
        stacked = lax.all_gather(stacked, name, axis=1, tiled=True)
    slab_count = stacked.shape[1] // rows_here
    stale_k = stacked[0].reshape(slab_count, rows_here, HEAD_DIM)
    stale_v = stacked[1].reshape(slab_count, rows_here, HEAD_DIM)

    fresh = jnp.stack([queries, fresh_keys, fresh_values]).reshape(
        3, rows_here, heads_here, HEAD_DIM
    )
    fresh = lax.all_to_all(fresh, "px", 2, 1, tiled=True).reshape(3, split, rows_here, HEAD_DIM)
    query_rows = fresh[0].reshape(split * rows_here, HEAD_DIM)

    score = (
        jnp.einsum("qd,skd->sqk", query_rows, stale_k, preferred_element_type=jnp.float32)
        * score_scale
    )
    block_max = jnp.max(score, axis=-1)
    weight = jnp.exp(score - block_max[..., None]).astype(jnp.bfloat16)
    block_num = jnp.einsum("sqk,skd->sqd", weight, stale_v, preferred_element_type=jnp.float32)
    block_den = jnp.sum(weight.astype(jnp.float32), axis=-1)

    home_score = (
        jnp.einsum("gqd,gkd->gqk", fresh[0], fresh[1], preferred_element_type=jnp.float32)
        * score_scale
    )
    home_max = jnp.max(home_score, axis=-1)
    home_weight = jnp.exp(home_score - home_max[..., None]).astype(jnp.bfloat16)
    home_num = jnp.einsum("gqk,gkd->gqd", home_weight, fresh[2], preferred_element_type=jnp.float32)
    home_den = jnp.sum(home_weight.astype(jnp.float32), axis=-1)
    home_max = home_max.reshape(1, split * rows_here)
    home_num = home_num.reshape(1, split * rows_here, HEAD_DIM)
    home_den = home_den.reshape(1, split * rows_here)

    first_slab = (device // split) * split
    query_slab = first_slab + jnp.arange(split * rows_here, dtype=jnp.int32) // rows_here
    is_home = jnp.arange(slab_count, dtype=jnp.int32)[:, None] == query_slab[None, :]
    block_max = jnp.where(is_home, home_max, block_max)
    block_den = jnp.where(is_home, home_den, block_den)
    block_num = jnp.where(is_home[..., None], home_num, block_num)

    top = jnp.max(block_max, axis=0)
    factor = jnp.exp(block_max - top[None, :])
    numer = jnp.sum(factor[..., None] * block_num, axis=0)
    denom = jnp.sum(factor * block_den, axis=0)
    result = (numer / denom[:, None]).astype(jnp.bfloat16)
    result = result.reshape(1, split, rows_here, HEAD_DIM)
    result = jnp.broadcast_to(result, (chan_count, split, rows_here, HEAD_DIM))
    result = result.reshape(chan_count * split, rows_here, HEAD_DIM)
    attended = lax.all_to_all(result, ("chan", "px"), 0, 0, tiled=True)
    attended = jnp.transpose(attended, (1, 0, 2)).reshape(rows_here, chan_count * inner)
    out_rows = lax.all_gather(w_out, "chan", axis=0, tiled=True)
    projected = jnp.dot(attended, out_rows, preferred_element_type=jnp.float32)
    projected = lax.dynamic_slice_in_dim(projected, lax.axis_index("chan") * chan_width, chan_width, axis=1)
    mixed = (latent.astype(jnp.float32) + projected).astype(jnp.bfloat16)
    return (mixed, fresh_keys, fresh_values)


def solution(mesh):
    devices = mesh.devices.reshape(PATCH_SPLIT + (mesh.shape["chan"],))
    split_mesh = Mesh(devices, PATCH_AXES + ("chan",))
    rows = PATCH_AXES
    in_specs = (
        P(rows, "chan"),
        P(),
        P("chan"),
        P("chan"),
        P(None, "chan"),
        P(None, "chan"),
        P(None, "chan"),
        P(None, "chan"),
        P("chan", None),
        P(rows, "chan"),
        P(rows, "chan"),
    )
    out_specs = (P(rows, "chan"), P(rows, "chan"), P(rows, "chan"))
    return jax.shard_map(
        local, mesh=split_mesh, in_specs=in_specs, out_specs=out_specs, check_vma=False
    )
```

```python
import math

import jax
import jax.numpy as jnp
from jax import lax
from jax.sharding import Mesh
from jax.sharding import PartitionSpec as P

D = 1280
HEAD_DIM = 64
GROUPS = 32
PATCH_AXES = ("py", "pz", "px")
PATCH_SPLIT = (8, 4, 4)


def timestep_shift(timestep, w_time):
    half_dim = w_time.shape[0] // 2
    frequency = jnp.exp(-math.log(10000.0) * jnp.arange(half_dim, dtype=jnp.float32) / half_dim)
    angles = timestep[0].astype(jnp.float32) * frequency
    embedding = jnp.concatenate([jnp.cos(angles), jnp.sin(angles)])
    return jnp.dot(
        jax.nn.silu(embedding)[None, :], w_time.astype(jnp.float32), precision=lax.Precision.HIGHEST
    )[0]


def patch_sum(partial):
    for name in reversed(PATCH_AXES):
        partial = lax.optimization_barrier(lax.psum(partial, name))
    return partial


def permute_gather(piece, name):
    size = lax.axis_size(name)
    here = lax.axis_index(name)
    received = [piece]
    for shift in range(1, size):
        pairs = [(source, (source + shift) % size) for source in range(size)]
        received.append(lax.ppermute(piece, name, pairs))
    received = jnp.stack(received)
    order = (here - jnp.arange(size, dtype=jnp.int32)) % size
    blocks = jnp.take(received, order, axis=0)
    blocks = jnp.moveaxis(blocks, 0, 1)
    return blocks.reshape(piece.shape[0], size * piece.shape[1], *piece.shape[2:])


def local(
    latent,
    timestep,
    norm_gain,
    norm_bias,
    w_time,
    w_query,
    w_key,
    w_value,
    w_out,
    stale_keys,
    stale_values,
):
    rows_here, chan_width = latent.shape
    patch_count = math.prod(lax.axis_size(name) for name in PATCH_AXES)
    chan_count = lax.axis_size("chan")
    device = lax.axis_index(PATCH_AXES)
    local_groups = GROUPS // chan_count
    width = D // GROUPS
    values = latent.astype(jnp.float32).reshape(rows_here, local_groups, width)
    count = rows_here * width
    group_mean = jnp.sum(values, axis=(0, 2)) / count
    spread = jnp.sum(jnp.square(values - group_mean[None, :, None]), axis=(0, 2))
    for name in reversed(PATCH_AXES):
        gathered = lax.all_gather(jnp.stack([group_mean, spread]), name)
        group_mean = jnp.mean(gathered[:, 0], axis=0)
        offset = gathered[:, 0] - group_mean[None, :]
        spread = jnp.sum(gathered[:, 1], axis=0) + count * jnp.sum(offset * offset, axis=0)
        count = count * gathered.shape[0]
    variance = spread / count
    centered = values - group_mean[None, :, None]
    scaled = (centered * lax.rsqrt(variance + 1e-05)[None, :, None]).reshape(rows_here, chan_width)
    normed = (scaled * norm_gain + norm_bias + timestep_shift(timestep, w_time)).astype(
        jnp.bfloat16
    )
    inner = w_query.shape[1]
    shard_piece = lax.all_gather(normed, "chan", axis=1, tiled=True)
    outputs = []
    for index, weight_matrix in enumerate((w_query, w_key, w_value)):
        outputs.append(jnp.dot(shard_piece, weight_matrix, preferred_element_type=jnp.float32))
    summed = tuple(outputs)
    queries = summed[0].astype(jnp.bfloat16)
    fresh_keys = summed[1].astype(jnp.bfloat16)
    fresh_values = summed[2].astype(jnp.bfloat16)
    heads_here = inner // HEAD_DIM
    score_scale = HEAD_DIM ** (-0.5)
    split = lax.axis_size("px")
    own_head = lax.axis_index("px")

    stacked = jnp.stack([stale_keys, stale_values]).reshape(2, rows_here, heads_here, HEAD_DIM)
    stacked = lax.all_to_all(stacked, "px", 2, 1, tiled=True).reshape(2, split * rows_here, HEAD_DIM)
    stacked = permute_gather(stacked, "pz")
    stacked = lax.all_gather(stacked, "py", axis=1, tiled=True)
    slab_count = stacked.shape[1] // rows_here
    stale_k = stacked[0].reshape(slab_count, rows_here, HEAD_DIM)
    stale_v = stacked[1].reshape(slab_count, rows_here, HEAD_DIM)

    fresh = jnp.stack([queries, fresh_keys, fresh_values]).reshape(
        3, rows_here, heads_here, HEAD_DIM
    )
    fresh = lax.all_to_all(fresh, "px", 2, 1, tiled=True).reshape(3, split, rows_here, HEAD_DIM)
    query_rows = fresh[0].reshape(split * rows_here, HEAD_DIM)

    score = (
        jnp.einsum("qd,skd->qsk", query_rows, stale_k, preferred_element_type=jnp.float32)
        * score_scale
    )
    block_max = jnp.max(score, axis=-1)
    weight = jnp.exp(score - block_max[..., None]).astype(jnp.bfloat16)
    block_num = jnp.einsum("qsk,skd->qsd", weight, stale_v, preferred_element_type=jnp.float32)
    block_den = jnp.sum(weight.astype(jnp.float32), axis=-1)

    home_score = (
        jnp.einsum("gqd,gkd->gqk", fresh[0], fresh[1], preferred_element_type=jnp.float32)
        * score_scale
    )
    home_max = jnp.max(home_score, axis=-1)
    home_weight = jnp.exp(home_score - home_max[..., None]).astype(jnp.bfloat16)
    home_num = jnp.einsum("gqk,gkd->gqd", home_weight, fresh[2], preferred_element_type=jnp.float32)
    home_den = jnp.sum(home_weight.astype(jnp.float32), axis=-1)
    home_max = home_max.reshape(split * rows_here, 1)
    home_num = home_num.reshape(split * rows_here, 1, HEAD_DIM)
    home_den = home_den.reshape(split * rows_here, 1)

    first_slab = (device // split) * split
    query_slab = first_slab + jnp.arange(split * rows_here, dtype=jnp.int32) // rows_here
    is_home = query_slab[:, None] == jnp.arange(slab_count, dtype=jnp.int32)[None, :]
    block_max = jnp.where(is_home, home_max, block_max)
    block_den = jnp.where(is_home, home_den, block_den)
    block_num = jnp.where(is_home[..., None], home_num, block_num)

    top = jnp.max(block_max, axis=-1)
    factor = jnp.exp(block_max - top[:, None])
    numer = jnp.sum(factor[..., None] * block_num, axis=1)
    denom = jnp.sum(factor * block_den, axis=1)
    result = (numer / denom[:, None]).astype(jnp.bfloat16)
    result = result.reshape(1, split, rows_here, HEAD_DIM)
    result = jnp.broadcast_to(result, (chan_count, split, rows_here, HEAD_DIM))
    result = result.reshape(chan_count * split, rows_here, HEAD_DIM)
    attended = lax.all_to_all(result, ("chan", "px"), 0, 0, tiled=True)
    attended = jnp.transpose(attended, (1, 0, 2)).reshape(rows_here, chan_count * inner)
    out_rows = lax.all_gather(w_out, "chan", axis=0, tiled=True)
    projected = jnp.dot(attended, out_rows, preferred_element_type=jnp.float32)
    projected = lax.dynamic_slice_in_dim(projected, lax.axis_index("chan") * chan_width, chan_width, axis=1)
    mixed = (latent.astype(jnp.float32) + projected).astype(jnp.bfloat16)
    return (mixed, fresh_keys, fresh_values)


def solution(mesh):
    devices = mesh.devices.reshape(PATCH_SPLIT + (mesh.shape["chan"],))
    split_mesh = Mesh(devices, PATCH_AXES + ("chan",))
    rows = PATCH_AXES
    in_specs = (
        P(rows, "chan"),
        P(),
        P("chan"),
        P("chan"),
        P(None, "chan"),
        P(None, "chan"),
        P(None, "chan"),
        P(None, "chan"),
        P("chan", None),
        P(rows, "chan"),
        P(rows, "chan"),
    )
    out_specs = (P(rows, "chan"), P(rows, "chan"), P(rows, "chan"))
    return jax.shard_map(
        local, mesh=split_mesh, in_specs=in_specs, out_specs=out_specs, check_vma=False
    )
```

```python
import math

import jax
import jax.numpy as jnp
from jax import lax
from jax.sharding import Mesh
from jax.sharding import PartitionSpec as P

D = 1280
HEAD_DIM = 64
GROUPS = 32
PATCH_AXES = ("py", "pz", "px")
PATCH_SPLIT = (8, 4, 4)


def timestep_shift(timestep, w_time):
    half_dim = w_time.shape[0] // 2
    frequency = jnp.exp(-math.log(10000.0) * jnp.arange(half_dim, dtype=jnp.float32) / half_dim)
    angles = timestep[0].astype(jnp.float32) * frequency
    embedding = jnp.concatenate([jnp.cos(angles), jnp.sin(angles)])
    return jnp.dot(
        jax.nn.silu(embedding)[None, :], w_time.astype(jnp.float32), precision=lax.Precision.HIGHEST
    )[0]


def patch_sum(partial):
    for name in reversed(PATCH_AXES):
        partial = lax.optimization_barrier(lax.psum(partial, name))
    return partial


def permute_gather(piece, name):
    size = lax.axis_size(name)
    here = lax.axis_index(name)
    received = [piece]
    for shift in range(1, size):
        pairs = [(source, (source + shift) % size) for source in range(size)]
        received.append(lax.ppermute(piece, name, pairs))
    received = jnp.stack(received)
    order = (here - jnp.arange(size, dtype=jnp.int32)) % size
    blocks = jnp.take(received, order, axis=0)
    blocks = jnp.moveaxis(blocks, 0, 1)
    return blocks.reshape(piece.shape[0], size * piece.shape[1], *piece.shape[2:])


def local(
    latent,
    timestep,
    norm_gain,
    norm_bias,
    w_time,
    w_query,
    w_key,
    w_value,
    w_out,
    stale_keys,
    stale_values,
):
    rows_here, chan_width = latent.shape
    patch_count = math.prod(lax.axis_size(name) for name in PATCH_AXES)
    chan_count = lax.axis_size("chan")
    device = lax.axis_index(PATCH_AXES)
    local_groups = GROUPS // chan_count
    width = D // GROUPS
    values = latent.astype(jnp.float32).reshape(rows_here, local_groups, width)
    count = rows_here * width
    group_mean = jnp.sum(values, axis=(0, 2)) / count
    spread = jnp.sum(jnp.square(values - group_mean[None, :, None]), axis=(0, 2))
    for name in reversed(PATCH_AXES):
        gathered = lax.all_gather(jnp.stack([group_mean, spread]), name)
        group_mean = jnp.mean(gathered[:, 0], axis=0)
        offset = gathered[:, 0] - group_mean[None, :]
        spread = jnp.sum(gathered[:, 1], axis=0) + count * jnp.sum(offset * offset, axis=0)
        count = count * gathered.shape[0]
    variance = spread / count
    centered = values - group_mean[None, :, None]
    scaled = (centered * lax.rsqrt(variance + 1e-05)[None, :, None]).reshape(rows_here, chan_width)
    normed = (scaled * norm_gain + norm_bias + timestep_shift(timestep, w_time)).astype(
        jnp.bfloat16
    )
    inner = w_query.shape[1]
    shard_piece = lax.all_gather(normed, "chan", axis=1, tiled=True)
    outputs = []
    for index, weight_matrix in enumerate((w_query, w_key, w_value)):
        outputs.append(jnp.dot(shard_piece, weight_matrix, preferred_element_type=jnp.float32))
    summed = tuple(outputs)
    queries = summed[0].astype(jnp.bfloat16)
    fresh_keys = summed[1].astype(jnp.bfloat16)
    fresh_values = summed[2].astype(jnp.bfloat16)
    heads_here = inner // HEAD_DIM
    score_scale = HEAD_DIM ** (-0.5)
    split = lax.axis_size("px")
    own_head = lax.axis_index("px")

    stacked = jnp.stack([stale_keys, stale_values]).reshape(2, rows_here, heads_here, HEAD_DIM)
    stacked = lax.all_to_all(stacked, "px", 2, 1, tiled=True).reshape(2, split * rows_here, HEAD_DIM)
    stacked = permute_gather(stacked, "pz")
    stacked = lax.all_gather(stacked, "py", axis=1, tiled=True)
    slab_count = stacked.shape[1] // rows_here

    fresh = jnp.stack([queries, fresh_keys, fresh_values]).reshape(
        3, rows_here, heads_here, HEAD_DIM
    )
    fresh = lax.all_to_all(fresh, "px", 2, 1, tiled=True).reshape(3, split, rows_here, HEAD_DIM)
    query_rows = fresh[0].reshape(split * rows_here, HEAD_DIM)

    key_rows = stacked[0]
    value_rows = stacked[1]
    score = (
        jnp.einsum("kd,qd->kq", key_rows, query_rows, preferred_element_type=jnp.float32)
        * score_scale
    ).reshape(slab_count, rows_here, split * rows_here)
    block_max = jnp.max(score, axis=1)
    weight = jnp.exp(score - block_max[:, None, :]).astype(jnp.bfloat16).astype(jnp.float32)

    home_score = (
        jnp.einsum("gqd,gkd->gqk", fresh[0], fresh[1], preferred_element_type=jnp.float32)
        * score_scale
    )
    home_max = jnp.max(home_score, axis=-1)
    home_weight = jnp.exp(home_score - home_max[..., None]).astype(jnp.bfloat16)
    home_num = jnp.einsum("gqk,gkd->gqd", home_weight, fresh[2], preferred_element_type=jnp.float32)
    home_den = jnp.sum(home_weight.astype(jnp.float32), axis=-1)
    home_max = home_max.reshape(split * rows_here)
    home_num = home_num.reshape(split * rows_here, HEAD_DIM)
    home_den = home_den.reshape(split * rows_here)

    first_slab = (device // split) * split
    query_slab = first_slab + jnp.arange(split * rows_here, dtype=jnp.int32) // rows_here
    is_home = jnp.arange(slab_count, dtype=jnp.int32)[:, None] == query_slab[None, :]
    block_max = jnp.where(is_home, home_max[None, :], block_max)
    top = jnp.max(block_max, axis=0)
    factor = jnp.exp(block_max - top[None, :])
    stale_factor = jnp.where(is_home, 0.0, factor)
    scaled_weight = (weight * stale_factor[:, None, :]).reshape(slab_count * rows_here, split * rows_here)
    stale_den = jnp.sum(scaled_weight, axis=0)
    stale_num = jnp.einsum(
        "kd,kq->qd", value_rows, scaled_weight.astype(jnp.bfloat16), preferred_element_type=jnp.float32
    )
    home_factor = jnp.exp(home_max - top)
    numer = stale_num + home_factor[:, None] * home_num
    denom = stale_den + home_factor * home_den
    result = (numer / denom[:, None]).astype(jnp.bfloat16)
    result = result.reshape(1, split, rows_here, HEAD_DIM)
    result = jnp.broadcast_to(result, (chan_count, split, rows_here, HEAD_DIM))
    result = result.reshape(chan_count * split, rows_here, HEAD_DIM)
    attended = lax.all_to_all(result, ("chan", "px"), 0, 0, tiled=True)
    attended = jnp.transpose(attended, (1, 0, 2)).reshape(rows_here, chan_count * inner)
    out_rows = lax.all_gather(w_out, "chan", axis=0, tiled=True)
    projected = jnp.dot(attended, out_rows, preferred_element_type=jnp.float32)
    projected = lax.dynamic_slice_in_dim(projected, lax.axis_index("chan") * chan_width, chan_width, axis=1)
    mixed = (latent.astype(jnp.float32) + projected).astype(jnp.bfloat16)
    return (mixed, fresh_keys, fresh_values)


def solution(mesh):
    devices = mesh.devices.reshape(PATCH_SPLIT + (mesh.shape["chan"],))
    split_mesh = Mesh(devices, PATCH_AXES + ("chan",))
    rows = PATCH_AXES
    in_specs = (
        P(rows, "chan"),
        P(),
        P("chan"),
        P("chan"),
        P(None, "chan"),
        P(None, "chan"),
        P(None, "chan"),
        P(None, "chan"),
        P("chan", None),
        P(rows, "chan"),
        P(rows, "chan"),
    )
    out_specs = (P(rows, "chan"), P(rows, "chan"), P(rows, "chan"))
    return jax.shard_map(
        local, mesh=split_mesh, in_specs=in_specs, out_specs=out_specs, check_vma=False
    )
```

```python
import math

import jax
import jax.numpy as jnp
from jax import lax
from jax.sharding import Mesh
from jax.sharding import PartitionSpec as P

D = 1280
HEAD_DIM = 64
GROUPS = 32
PATCH_AXES = ("py", "pz", "px")
PATCH_SPLIT = (8, 4, 4)


def timestep_shift(timestep, w_time):
    half_dim = w_time.shape[0] // 2
    frequency = jnp.exp(-math.log(10000.0) * jnp.arange(half_dim, dtype=jnp.float32) / half_dim)
    angles = timestep[0].astype(jnp.float32) * frequency
    embedding = jnp.concatenate([jnp.cos(angles), jnp.sin(angles)])
    return jnp.dot(
        jax.nn.silu(embedding)[None, :], w_time.astype(jnp.float32), precision=lax.Precision.HIGHEST
    )[0]


def patch_sum(partial):
    for name in reversed(PATCH_AXES):
        partial = lax.optimization_barrier(lax.psum(partial, name))
    return partial


def replicated_gather(piece, name):
    size = lax.axis_size(name)
    if size <= 4:
        return lax.all_gather(piece, name)
    copies = jnp.broadcast_to(piece[None], (size,) + piece.shape)
    return lax.all_to_all(copies, name, 0, 0, tiled=True)


def permute_gather(piece, name):
    size = lax.axis_size(name)
    here = lax.axis_index(name)
    received = [piece]
    for shift in range(1, size):
        pairs = [(source, (source + shift) % size) for source in range(size)]
        received.append(lax.ppermute(piece, name, pairs))
    received = jnp.stack(received)
    order = (here - jnp.arange(size, dtype=jnp.int32)) % size
    blocks = jnp.take(received, order, axis=0)
    blocks = jnp.moveaxis(blocks, 0, 1)
    return blocks.reshape(piece.shape[0], size * piece.shape[1], *piece.shape[2:])


def local(
    latent,
    timestep,
    norm_gain,
    norm_bias,
    w_time,
    w_query,
    w_key,
    w_value,
    w_out,
    stale_keys,
    stale_values,
):
    rows_here, chan_width = latent.shape
    patch_count = math.prod(lax.axis_size(name) for name in PATCH_AXES)
    chan_count = lax.axis_size("chan")
    device = lax.axis_index(PATCH_AXES)
    local_groups = GROUPS // chan_count
    width = D // GROUPS
    values = latent.astype(jnp.float32).reshape(rows_here, local_groups, width)
    count = rows_here * width
    group_mean = jnp.sum(values, axis=(0, 2)) / count
    spread = jnp.sum(jnp.square(values - group_mean[None, :, None]), axis=(0, 2))
    for name in reversed(PATCH_AXES):
        gathered = replicated_gather(jnp.stack([group_mean, spread]), name)
        group_mean = jnp.mean(gathered[:, 0], axis=0)
        offset = gathered[:, 0] - group_mean[None, :]
        spread = jnp.sum(gathered[:, 1], axis=0) + count * jnp.sum(offset * offset, axis=0)
        count = count * gathered.shape[0]
    variance = spread / count
    centered = values - group_mean[None, :, None]
    scaled = (centered * lax.rsqrt(variance + 1e-05)[None, :, None]).reshape(rows_here, chan_width)
    normed = (scaled * norm_gain + norm_bias + timestep_shift(timestep, w_time)).astype(
        jnp.bfloat16
    )
    inner = w_query.shape[1]
    shard_piece = lax.all_gather(normed, "chan", axis=1, tiled=True)
    outputs = []
    for index, weight_matrix in enumerate((w_query, w_key, w_value)):
        outputs.append(jnp.dot(shard_piece, weight_matrix, preferred_element_type=jnp.float32))
    summed = tuple(outputs)
    queries = summed[0].astype(jnp.bfloat16)
    fresh_keys = summed[1].astype(jnp.bfloat16)
    fresh_values = summed[2].astype(jnp.bfloat16)
    heads_here = inner // HEAD_DIM
    score_scale = HEAD_DIM ** (-0.5)
    split = lax.axis_size("px")
    own_head = lax.axis_index("px")

    stacked = jnp.stack([stale_keys, stale_values]).reshape(2, rows_here, heads_here, HEAD_DIM)
    stacked = lax.all_to_all(stacked, "px", 2, 1, tiled=True).reshape(2, split * rows_here, HEAD_DIM)
    stacked = permute_gather(stacked, "pz")
    stacked = lax.all_gather(stacked, "py", axis=1, tiled=True)
    slab_count = stacked.shape[1] // rows_here

    fresh = jnp.stack([queries, fresh_keys, fresh_values]).reshape(
        3, rows_here, heads_here, HEAD_DIM
    )
    fresh = lax.all_to_all(fresh, "px", 2, 1, tiled=True).reshape(3, split, rows_here, HEAD_DIM)
    query_rows = fresh[0].reshape(split * rows_here, HEAD_DIM)

    key_rows = stacked[0]
    value_rows = stacked[1]
    score = (
        jnp.einsum("kd,qd->kq", key_rows, query_rows, preferred_element_type=jnp.float32)
        * score_scale
    ).reshape(slab_count, rows_here, split * rows_here)
    block_max = jnp.max(score, axis=1)
    weight = jnp.exp(score - block_max[:, None, :]).astype(jnp.bfloat16).astype(jnp.float32)

    home_score = (
        jnp.einsum("gqd,gkd->gqk", fresh[0], fresh[1], preferred_element_type=jnp.float32)
        * score_scale
    )
    home_max = jnp.max(home_score, axis=-1)
    home_weight = jnp.exp(home_score - home_max[..., None]).astype(jnp.bfloat16)
    home_num = jnp.einsum("gqk,gkd->gqd", home_weight, fresh[2], preferred_element_type=jnp.float32)
    home_den = jnp.sum(home_weight.astype(jnp.float32), axis=-1)
    home_max = home_max.reshape(split * rows_here)
    home_num = home_num.reshape(split * rows_here, HEAD_DIM)
    home_den = home_den.reshape(split * rows_here)

    first_slab = (device // split) * split
    query_slab = first_slab + jnp.arange(split * rows_here, dtype=jnp.int32) // rows_here
    is_home = jnp.arange(slab_count, dtype=jnp.int32)[:, None] == query_slab[None, :]
    block_max = jnp.where(is_home, home_max[None, :], block_max)
    top = jnp.max(block_max, axis=0)
    factor = jnp.exp(block_max - top[None, :])
    stale_factor = jnp.where(is_home, 0.0, factor)
    scaled_weight = (weight * stale_factor[:, None, :]).reshape(slab_count * rows_here, split * rows_here)
    scaled_weight = scaled_weight.astype(jnp.bfloat16)
    stale_den = jnp.sum(scaled_weight.astype(jnp.float32), axis=0)
    stale_num = jnp.einsum(
        "kd,kq->qd", value_rows, scaled_weight, preferred_element_type=jnp.float32
    )
    home_factor = jnp.exp(home_max - top)
    numer = stale_num + home_factor[:, None] * home_num
    denom = stale_den + home_factor * home_den
    result = (numer / denom[:, None]).astype(jnp.bfloat16)
    result = result.reshape(1, split, rows_here, HEAD_DIM)
    result = jnp.broadcast_to(result, (chan_count, split, rows_here, HEAD_DIM))
    result = result.reshape(chan_count * split, rows_here, HEAD_DIM)
    attended = lax.all_to_all(result, ("chan", "px"), 0, 0, tiled=True)
    attended = jnp.transpose(attended, (1, 0, 2)).reshape(rows_here, chan_count * inner)
    out_columns = lax.all_to_all(w_out, "chan", 1, 0, tiled=True)
    projected = jnp.dot(attended, out_columns, preferred_element_type=jnp.float32)
    mixed = (latent.astype(jnp.float32) + projected).astype(jnp.bfloat16)
    return (mixed, fresh_keys, fresh_values)


def solution(mesh):
    devices = mesh.devices.reshape(PATCH_SPLIT + (mesh.shape["chan"],))
    split_mesh = Mesh(devices, PATCH_AXES + ("chan",))
    rows = PATCH_AXES
    in_specs = (
        P(rows, "chan"),
        P(),
        P("chan"),
        P("chan"),
        P(None, "chan"),
        P(None, "chan"),
        P(None, "chan"),
        P(None, "chan"),
        P("chan", None),
        P(rows, "chan"),
        P(rows, "chan"),
    )
    out_specs = (P(rows, "chan"), P(rows, "chan"), P(rows, "chan"))
    return jax.shard_map(
        local, mesh=split_mesh, in_specs=in_specs, out_specs=out_specs, check_vma=False
    )
```

```python
import math

import jax
import jax.numpy as jnp
from jax import lax
from jax.sharding import Mesh
from jax.sharding import PartitionSpec as P

D = 1280
HEAD_DIM = 64
GROUPS = 32
PATCH_AXES = ("py", "pz", "px")
PATCH_SPLIT = (8, 4, 4)


def timestep_shift(timestep, w_time):
    half_dim = w_time.shape[0] // 2
    frequency = jnp.exp(-math.log(10000.0) * jnp.arange(half_dim, dtype=jnp.float32) / half_dim)
    angles = timestep[0].astype(jnp.float32) * frequency
    embedding = jnp.concatenate([jnp.cos(angles), jnp.sin(angles)])
    return jnp.dot(
        jax.nn.silu(embedding)[None, :], w_time.astype(jnp.float32), precision=lax.Precision.HIGHEST
    )[0]


def patch_sum(partial):
    for name in reversed(PATCH_AXES):
        partial = lax.optimization_barrier(lax.psum(partial, name))
    return partial


def replicated_gather(piece, name):
    size = lax.axis_size(name)
    copies = jnp.broadcast_to(piece[None], (size,) + piece.shape)
    return lax.all_to_all(copies, name, 0, 0, tiled=True)


def permute_gather(piece, name):
    size = lax.axis_size(name)
    here = lax.axis_index(name)
    received = [piece]
    for shift in range(1, size):
        pairs = [(source, (source + shift) % size) for source in range(size)]
        received.append(lax.ppermute(piece, name, pairs))
    received = jnp.stack(received)
    order = (here - jnp.arange(size, dtype=jnp.int32)) % size
    blocks = jnp.take(received, order, axis=0)
    blocks = jnp.moveaxis(blocks, 0, 1)
    return blocks.reshape(piece.shape[0], size * piece.shape[1], *piece.shape[2:])


def local(
    latent,
    timestep,
    norm_gain,
    norm_bias,
    w_time,
    w_query,
    w_key,
    w_value,
    w_out,
    stale_keys,
    stale_values,
):
    rows_here, chan_width = latent.shape
    patch_count = math.prod(lax.axis_size(name) for name in PATCH_AXES)
    chan_count = lax.axis_size("chan")
    device = lax.axis_index(PATCH_AXES)
    local_groups = GROUPS // chan_count
    width = D // GROUPS
    values = latent.astype(jnp.float32).reshape(rows_here, local_groups, width)
    count = rows_here * width
    group_mean = jnp.sum(values, axis=(0, 2)) / count
    spread = jnp.sum(jnp.square(values - group_mean[None, :, None]), axis=(0, 2))
    for name in (PATCH_AXES[1:], PATCH_AXES[0]):
        gathered = replicated_gather(jnp.stack([group_mean, spread]), name)
        group_mean = jnp.mean(gathered[:, 0], axis=0)
        offset = gathered[:, 0] - group_mean[None, :]
        spread = jnp.sum(gathered[:, 1], axis=0) + count * jnp.sum(offset * offset, axis=0)
        count = count * gathered.shape[0]
    variance = spread / count
    centered = values - group_mean[None, :, None]
    scaled = (centered * lax.rsqrt(variance + 1e-05)[None, :, None]).reshape(rows_here, chan_width)
    normed = (scaled * norm_gain + norm_bias + timestep_shift(timestep, w_time)).astype(
        jnp.bfloat16
    )
    inner = w_query.shape[1]
    shard_piece = lax.all_gather(normed, "chan", axis=1, tiled=True)
    outputs = []
    for index, weight_matrix in enumerate((w_query, w_key, w_value)):
        outputs.append(jnp.dot(shard_piece, weight_matrix, preferred_element_type=jnp.float32))
    summed = tuple(outputs)
    queries = summed[0].astype(jnp.bfloat16)
    fresh_keys = summed[1].astype(jnp.bfloat16)
    fresh_values = summed[2].astype(jnp.bfloat16)
    heads_here = inner // HEAD_DIM
    score_scale = HEAD_DIM ** (-0.5)
    split = lax.axis_size("px")
    own_head = lax.axis_index("px")

    stacked = jnp.stack([stale_keys, stale_values]).reshape(2, rows_here, heads_here, HEAD_DIM)
    stacked = lax.all_to_all(stacked, "px", 2, 1, tiled=True).reshape(2, split * rows_here, HEAD_DIM)
    stacked = jnp.moveaxis(replicated_gather(stacked, "pz"), 0, 1).reshape(2, -1, HEAD_DIM)
    stacked = lax.all_gather(stacked, "py", axis=1, tiled=True)
    slab_count = stacked.shape[1] // rows_here

    fresh = jnp.stack([queries, fresh_keys, fresh_values]).reshape(
        3, rows_here, heads_here, HEAD_DIM
    )
    fresh = lax.all_to_all(fresh, "px", 2, 1, tiled=True).reshape(3, split, rows_here, HEAD_DIM)
    query_rows = fresh[0].reshape(split * rows_here, HEAD_DIM)

    key_rows = stacked[0]
    value_rows = stacked[1]
    score = (
        jnp.einsum("kd,qd->kq", key_rows, query_rows, preferred_element_type=jnp.float32)
        * score_scale
    ).reshape(slab_count, rows_here, split * rows_here)
    block_max = jnp.max(score, axis=1)
    weight = jnp.exp(score - block_max[:, None, :]).astype(jnp.bfloat16).astype(jnp.float32)

    home_score = (
        jnp.einsum("gqd,gkd->gqk", fresh[0], fresh[1], preferred_element_type=jnp.float32)
        * score_scale
    )
    home_max = jnp.max(home_score, axis=-1)
    home_weight = jnp.exp(home_score - home_max[..., None]).astype(jnp.bfloat16)
    home_num = jnp.einsum("gqk,gkd->gqd", home_weight, fresh[2], preferred_element_type=jnp.float32)
    home_den = jnp.sum(home_weight.astype(jnp.float32), axis=-1)
    home_max = home_max.reshape(split * rows_here)
    home_num = home_num.reshape(split * rows_here, HEAD_DIM)
    home_den = home_den.reshape(split * rows_here)

    first_slab = (device // split) * split
    query_slab = first_slab + jnp.arange(split * rows_here, dtype=jnp.int32) // rows_here
    is_home = jnp.arange(slab_count, dtype=jnp.int32)[:, None] == query_slab[None, :]
    block_max = jnp.where(is_home, home_max[None, :], block_max)
    top = jnp.max(block_max, axis=0)
    factor = jnp.exp(block_max - top[None, :])
    stale_factor = jnp.where(is_home, 0.0, factor)
    scaled_weight = (weight * stale_factor[:, None, :]).reshape(slab_count * rows_here, split * rows_here)
    scaled_weight = scaled_weight.astype(jnp.bfloat16)
    stale_den = jnp.sum(scaled_weight.astype(jnp.float32), axis=0)
    stale_num = jnp.einsum(
        "kd,kq->qd", value_rows, scaled_weight, preferred_element_type=jnp.float32
    )
    home_factor = jnp.exp(home_max - top)
    numer = stale_num + home_factor[:, None] * home_num
    denom = stale_den + home_factor * home_den
    result = (numer / denom[:, None]).astype(jnp.bfloat16)
    result = result.reshape(1, split, rows_here, HEAD_DIM)
    result = jnp.broadcast_to(result, (chan_count, split, rows_here, HEAD_DIM))
    result = result.reshape(chan_count * split, rows_here, HEAD_DIM)
    attended = lax.all_to_all(result, ("chan", "px"), 0, 0, tiled=True)
    attended = jnp.transpose(attended, (1, 0, 2)).reshape(rows_here, chan_count * inner)
    out_columns = lax.all_to_all(w_out, "chan", 1, 0, tiled=True)
    projected = jnp.dot(attended, out_columns, preferred_element_type=jnp.float32)
    mixed = (latent.astype(jnp.float32) + projected).astype(jnp.bfloat16)
    return (mixed, fresh_keys, fresh_values)


def solution(mesh):
    devices = mesh.devices.reshape(PATCH_SPLIT + (mesh.shape["chan"],))
    split_mesh = Mesh(devices, PATCH_AXES + ("chan",))
    rows = PATCH_AXES
    in_specs = (
        P(rows, "chan"),
        P(),
        P("chan"),
        P("chan"),
        P(None, "chan"),
        P(None, "chan"),
        P(None, "chan"),
        P(None, "chan"),
        P("chan", None),
        P(rows, "chan"),
        P(rows, "chan"),
    )
    out_specs = (P(rows, "chan"), P(rows, "chan"), P(rows, "chan"))
    return jax.shard_map(
        local, mesh=split_mesh, in_specs=in_specs, out_specs=out_specs, check_vma=False
    )
```

```python
import math

import jax
import jax.numpy as jnp
from jax import lax
from jax.sharding import Mesh
from jax.sharding import PartitionSpec as P

D = 1280
HEAD_DIM = 64
GROUPS = 32
PATCH_AXES = ("py", "pz", "px")
PATCH_SPLIT = (8, 4, 4)


def timestep_shift(timestep, w_time):
    half_dim = w_time.shape[0] // 2
    frequency = jnp.exp(-math.log(10000.0) * jnp.arange(half_dim, dtype=jnp.float32) / half_dim)
    angles = timestep[0].astype(jnp.float32) * frequency
    embedding = jnp.concatenate([jnp.cos(angles), jnp.sin(angles)])
    return jnp.dot(
        jax.nn.silu(embedding)[None, :], w_time.astype(jnp.float32), precision=lax.Precision.HIGHEST
    )[0]


def replicated_gather(piece, name):
    size = lax.axis_size(name)
    copies = jnp.broadcast_to(piece[None], (size,) + piece.shape)
    return lax.all_to_all(copies, name, 0, 0, tiled=True)


def permute_columns(rows, name, width):
    size = lax.axis_size(name)
    here = lax.axis_index(name)
    received = [lax.dynamic_slice_in_dim(rows, here * width, width, axis=1)]
    for shift in range(1, size):
        pairs = [(source, (source + shift) % size) for source in range(size)]
        chunk = lax.dynamic_slice_in_dim(rows, ((here + shift) % size) * width, width, axis=1)
        received.append(lax.ppermute(chunk, name, pairs))
    received = jnp.stack(received)
    order = (here - jnp.arange(size, dtype=jnp.int32)) % size
    return jnp.take(received, order, axis=0).reshape(size * rows.shape[0], width)


def local(
    latent,
    timestep,
    norm_gain,
    norm_bias,
    w_time,
    w_query,
    w_key,
    w_value,
    w_out,
    stale_keys,
    stale_values,
):
    rows_here, chan_width = latent.shape
    chan_count = lax.axis_size("chan")
    device = lax.axis_index(PATCH_AXES)
    local_groups = GROUPS // chan_count
    width = D // GROUPS
    values = latent.astype(jnp.float32).reshape(rows_here, local_groups, width)
    count = rows_here * width
    group_mean = jnp.sum(values, axis=(0, 2)) / count
    spread = jnp.sum(jnp.square(values - group_mean[None, :, None]), axis=(0, 2))
    for name in (PATCH_AXES[1:], PATCH_AXES[0]):
        gathered = replicated_gather(jnp.stack([group_mean, spread]), name)
        group_mean = jnp.mean(gathered[:, 0], axis=0)
        offset = gathered[:, 0] - group_mean[None, :]
        spread = jnp.sum(gathered[:, 1], axis=0) + count * jnp.sum(offset * offset, axis=0)
        count = count * gathered.shape[0]
    variance = spread / count
    centered = values - group_mean[None, :, None]
    scaled = (centered * lax.rsqrt(variance + 1e-05)[None, :, None]).reshape(rows_here, chan_width)
    normed = (scaled * norm_gain + norm_bias + timestep_shift(timestep, w_time)).astype(
        jnp.bfloat16
    )
    inner = w_query.shape[1]
    shard_piece = lax.all_gather(normed, "chan", axis=1, tiled=True)
    outputs = []
    for weight_matrix in (w_query, w_key, w_value):
        outputs.append(jnp.dot(shard_piece, weight_matrix, preferred_element_type=jnp.float32))
    summed = tuple(outputs)
    queries = summed[0].astype(jnp.bfloat16)
    fresh_keys = summed[1].astype(jnp.bfloat16)
    fresh_values = summed[2].astype(jnp.bfloat16)
    heads_here = inner // HEAD_DIM
    score_scale = HEAD_DIM ** (-0.5)
    split = lax.axis_size("px")

    stacked = jnp.stack([stale_keys, stale_values]).reshape(2, rows_here, heads_here, HEAD_DIM)
    stacked = lax.all_to_all(stacked, "px", 2, 1, tiled=True).reshape(2, split * rows_here, HEAD_DIM)
    stacked = jnp.moveaxis(replicated_gather(stacked, "pz"), 0, 1).reshape(2, -1, HEAD_DIM)
    stacked = lax.all_gather(stacked, "py", axis=1, tiled=True)
    slab_count = stacked.shape[1] // rows_here

    fresh = jnp.stack([queries, fresh_keys, fresh_values]).reshape(
        3, rows_here, heads_here, HEAD_DIM
    )
    fresh = lax.all_to_all(fresh, "px", 2, 1, tiled=True).reshape(3, split, rows_here, HEAD_DIM)
    query_rows = fresh[0].reshape(split * rows_here, HEAD_DIM)

    key_rows = stacked[0]
    value_rows = stacked[1]
    score = (
        jnp.einsum("kd,qd->kq", key_rows, query_rows, preferred_element_type=jnp.float32)
        * score_scale
    ).reshape(slab_count, rows_here, split * rows_here)
    block_max = jnp.max(score, axis=1)
    weight = jnp.exp(score - block_max[:, None, :]).astype(jnp.bfloat16).astype(jnp.float32)

    home_score = (
        jnp.einsum("gqd,gkd->gqk", fresh[0], fresh[1], preferred_element_type=jnp.float32)
        * score_scale
    )
    home_max = jnp.max(home_score, axis=-1)
    home_weight = jnp.exp(home_score - home_max[..., None]).astype(jnp.bfloat16)
    home_num = jnp.einsum("gqk,gkd->gqd", home_weight, fresh[2], preferred_element_type=jnp.float32)
    home_den = jnp.sum(home_weight.astype(jnp.float32), axis=-1)
    home_max = home_max.reshape(split * rows_here)
    home_num = home_num.reshape(split * rows_here, HEAD_DIM)
    home_den = home_den.reshape(split * rows_here)

    first_slab = (device // split) * split
    query_slab = first_slab + jnp.arange(split * rows_here, dtype=jnp.int32) // rows_here
    is_home = jnp.arange(slab_count, dtype=jnp.int32)[:, None] == query_slab[None, :]
    block_max = jnp.where(is_home, home_max[None, :], block_max)
    top = jnp.max(block_max, axis=0)
    factor = jnp.exp(block_max - top[None, :])
    stale_factor = jnp.where(is_home, 0.0, factor)
    scaled_weight = (weight * stale_factor[:, None, :]).reshape(slab_count * rows_here, split * rows_here)
    scaled_weight = scaled_weight.astype(jnp.bfloat16)
    stale_den = jnp.sum(scaled_weight.astype(jnp.float32), axis=0)
    stale_num = jnp.einsum(
        "kd,kq->qd", value_rows, scaled_weight, preferred_element_type=jnp.float32
    )
    home_factor = jnp.exp(home_max - top)
    numer = stale_num + home_factor[:, None] * home_num
    denom = stale_den + home_factor * home_den
    result = (numer / denom[:, None]).astype(jnp.bfloat16)
    result = result.reshape(1, split, rows_here, HEAD_DIM)
    result = jnp.broadcast_to(result, (chan_count, split, rows_here, HEAD_DIM))
    result = result.reshape(chan_count * split, rows_here, HEAD_DIM)
    attended = lax.all_to_all(result, ("chan", "px"), 0, 0, tiled=True)
    attended = jnp.transpose(attended, (1, 0, 2)).reshape(rows_here, chan_count * inner)
    out_columns = permute_columns(w_out, "chan", chan_width)
    projected = jnp.dot(attended, out_columns, preferred_element_type=jnp.float32)
    mixed = (latent.astype(jnp.float32) + projected).astype(jnp.bfloat16)
    return (mixed, fresh_keys, fresh_values)


def solution(mesh):
    devices = mesh.devices.reshape(PATCH_SPLIT + (mesh.shape["chan"],))
    split_mesh = Mesh(devices, PATCH_AXES + ("chan",))
    rows = PATCH_AXES
    in_specs = (
        P(rows, "chan"),
        P(),
        P("chan"),
        P("chan"),
        P(None, "chan"),
        P(None, "chan"),
        P(None, "chan"),
        P(None, "chan"),
        P("chan", None),
        P(rows, "chan"),
        P(rows, "chan"),
    )
    out_specs = (P(rows, "chan"), P(rows, "chan"), P(rows, "chan"))

    return jax.shard_map(
        local, mesh=split_mesh, in_specs=in_specs, out_specs=out_specs, check_vma=False
    )
```

```python
import math

import jax
import jax.numpy as jnp
from jax import lax
from jax.sharding import Mesh
from jax.sharding import PartitionSpec as P

D = 1280
HEAD_DIM = 64
GROUPS = 32
PATCH_AXES = ("py", "pz", "px")
PATCH_SPLIT = (8, 4, 4)


def timestep_shift(timestep, w_time):
    half_dim = w_time.shape[0] // 2
    frequency = jnp.exp(-math.log(10000.0) * jnp.arange(half_dim, dtype=jnp.float32) / half_dim)
    angles = timestep[0].astype(jnp.float32) * frequency
    embedding = jnp.concatenate([jnp.cos(angles), jnp.sin(angles)])
    return jnp.dot(
        jax.nn.silu(embedding)[None, :], w_time.astype(jnp.float32), precision=lax.Precision.HIGHEST
    )[0]


def patch_sum(partial):
    for name in reversed(PATCH_AXES):
        partial = lax.optimization_barrier(lax.psum(partial, name))
    return partial


def replicated_gather(piece, name):
    size = lax.axis_size(name)
    copies = jnp.broadcast_to(piece[None], (size,) + piece.shape)
    return lax.all_to_all(copies, name, 0, 0, tiled=True)


def permute_gather(piece, name):
    size = lax.axis_size(name)
    here = lax.axis_index(name)
    received = [piece]
    for shift in range(1, size):
        pairs = [(source, (source + shift) % size) for source in range(size)]
        received.append(lax.ppermute(piece, name, pairs))
    received = jnp.stack(received)
    order = (here - jnp.arange(size, dtype=jnp.int32)) % size
    blocks = jnp.take(received, order, axis=0)
    blocks = jnp.moveaxis(blocks, 0, 1)
    return blocks.reshape(piece.shape[0], size * piece.shape[1], *piece.shape[2:])


def local(
    latent,
    timestep,
    norm_gain,
    norm_bias,
    w_time,
    w_query,
    w_key,
    w_value,
    w_out,
    stale_keys,
    stale_values,
):
    rows_here, chan_width = latent.shape
    patch_count = math.prod(lax.axis_size(name) for name in PATCH_AXES)
    chan_count = lax.axis_size("chan")
    device = lax.axis_index(PATCH_AXES)
    local_groups = GROUPS // chan_count
    width = D // GROUPS
    values = latent.astype(jnp.float32).reshape(rows_here, local_groups, width)
    count = rows_here * width
    group_mean = jnp.sum(values, axis=(0, 2)) / count
    spread = jnp.sum(jnp.square(values - group_mean[None, :, None]), axis=(0, 2))
    for name in (PATCH_AXES,):
        gathered = replicated_gather(jnp.stack([group_mean, spread]), name)
        group_mean = jnp.mean(gathered[:, 0], axis=0)
        offset = gathered[:, 0] - group_mean[None, :]
        spread = jnp.sum(gathered[:, 1], axis=0) + count * jnp.sum(offset * offset, axis=0)
        count = count * gathered.shape[0]
    variance = spread / count
    centered = values - group_mean[None, :, None]
    scaled = (centered * lax.rsqrt(variance + 1e-05)[None, :, None]).reshape(rows_here, chan_width)
    normed = (scaled * norm_gain + norm_bias + timestep_shift(timestep, w_time)).astype(
        jnp.bfloat16
    )
    inner = w_query.shape[1]
    shard_piece = replicated_gather(normed, "chan")
    shard_piece = jnp.moveaxis(shard_piece, 0, 1).reshape(rows_here, chan_count * chan_width)
    outputs = []
    for index, weight_matrix in enumerate((w_query, w_key, w_value)):
        outputs.append(jnp.dot(shard_piece, weight_matrix, preferred_element_type=jnp.float32))
    summed = tuple(outputs)
    queries = summed[0].astype(jnp.bfloat16)
    fresh_keys = summed[1].astype(jnp.bfloat16)
    fresh_values = summed[2].astype(jnp.bfloat16)
    heads_here = inner // HEAD_DIM
    score_scale = HEAD_DIM ** (-0.5)
    split = lax.axis_size("px")
    own_head = lax.axis_index("px")

    stacked = jnp.stack([stale_keys, stale_values]).reshape(2, rows_here, heads_here, HEAD_DIM)
    stacked = lax.all_to_all(stacked, "px", 2, 1, tiled=True).reshape(2, split * rows_here, HEAD_DIM)
    stacked = jnp.moveaxis(replicated_gather(stacked, "pz"), 0, 1).reshape(2, -1, HEAD_DIM)
    stacked = lax.all_gather(stacked, "py", axis=1, tiled=True)
    slab_count = stacked.shape[1] // rows_here

    fresh = jnp.stack([queries, fresh_keys, fresh_values]).reshape(
        3, rows_here, heads_here, HEAD_DIM
    )
    fresh = lax.all_to_all(fresh, "px", 2, 1, tiled=True).reshape(3, split, rows_here, HEAD_DIM)
    query_rows = fresh[0].reshape(split * rows_here, HEAD_DIM)

    key_rows = stacked[0]
    value_rows = stacked[1]
    score = (
        jnp.einsum("kd,qd->kq", key_rows, query_rows, preferred_element_type=jnp.float32)
        * score_scale
    ).reshape(slab_count, rows_here, split * rows_here)
    block_max = jnp.max(score, axis=1)
    weight = jnp.exp(score - block_max[:, None, :]).astype(jnp.bfloat16).astype(jnp.float32)

    home_score = (
        jnp.einsum("gqd,gkd->gqk", fresh[0], fresh[1], preferred_element_type=jnp.float32)
        * score_scale
    )
    home_max = jnp.max(home_score, axis=-1)
    home_weight = jnp.exp(home_score - home_max[..., None]).astype(jnp.bfloat16)
    home_num = jnp.einsum("gqk,gkd->gqd", home_weight, fresh[2], preferred_element_type=jnp.float32)
    home_den = jnp.sum(home_weight.astype(jnp.float32), axis=-1)
    home_max = home_max.reshape(split * rows_here)
    home_num = home_num.reshape(split * rows_here, HEAD_DIM)
    home_den = home_den.reshape(split * rows_here)

    first_slab = (device // split) * split
    query_slab = first_slab + jnp.arange(split * rows_here, dtype=jnp.int32) // rows_here
    is_home = jnp.arange(slab_count, dtype=jnp.int32)[:, None] == query_slab[None, :]
    block_max = jnp.where(is_home, home_max[None, :], block_max)
    top = jnp.max(block_max, axis=0)
    factor = jnp.exp(block_max - top[None, :])
    stale_factor = jnp.where(is_home, 0.0, factor)
    scaled_weight = (weight * stale_factor[:, None, :]).reshape(slab_count * rows_here, split * rows_here)
    scaled_weight = scaled_weight.astype(jnp.bfloat16)
    stale_den = jnp.sum(scaled_weight.astype(jnp.float32), axis=0)
    stale_num = jnp.einsum(
        "kd,kq->qd", value_rows, scaled_weight, preferred_element_type=jnp.float32
    )
    home_factor = jnp.exp(home_max - top)
    numer = stale_num + home_factor[:, None] * home_num
    denom = stale_den + home_factor * home_den
    result = (numer / denom[:, None]).astype(jnp.bfloat16)
    result = result.reshape(1, split, rows_here, HEAD_DIM)
    result = jnp.broadcast_to(result, (chan_count, split, rows_here, HEAD_DIM))
    result = result.reshape(chan_count * split, rows_here, HEAD_DIM)
    attended = lax.all_to_all(result, ("chan", "px"), 0, 0, tiled=True)
    attended = jnp.transpose(attended, (1, 0, 2)).reshape(rows_here, chan_count * inner)
    out_columns = lax.all_to_all(w_out, "chan", 1, 0, tiled=True)
    projected = jnp.dot(attended, out_columns, preferred_element_type=jnp.float32)
    mixed = (latent.astype(jnp.float32) + projected).astype(jnp.bfloat16)
    return (mixed, fresh_keys, fresh_values)


def solution(mesh):
    devices = mesh.devices.reshape(PATCH_SPLIT + (mesh.shape["chan"],))
    split_mesh = Mesh(devices, PATCH_AXES + ("chan",))
    rows = PATCH_AXES
    in_specs = (
        P(rows, "chan"),
        P(),
        P("chan"),
        P("chan"),
        P(None, "chan"),
        P(None, "chan"),
        P(None, "chan"),
        P(None, "chan"),
        P("chan", None),
        P(rows, "chan"),
        P(rows, "chan"),
    )
    out_specs = (P(rows, "chan"), P(rows, "chan"), P(rows, "chan"))
    return jax.shard_map(
        local, mesh=split_mesh, in_specs=in_specs, out_specs=out_specs, check_vma=False
    )
```

```python
import math

import jax
import jax.numpy as jnp
from jax import lax
from jax.sharding import Mesh
from jax.sharding import PartitionSpec as P

D = 1280
HEAD_DIM = 64
GROUPS = 32
PATCH_AXES = ("py", "pz", "px")
PATCH_SPLIT = (8, 4, 4)


def timestep_shift(timestep, w_time):
    half_dim = w_time.shape[0] // 2
    frequency = jnp.exp(-math.log(10000.0) * jnp.arange(half_dim, dtype=jnp.float32) / half_dim)
    angles = timestep[0].astype(jnp.float32) * frequency
    embedding = jnp.concatenate([jnp.cos(angles), jnp.sin(angles)])
    return jnp.dot(
        jax.nn.silu(embedding)[None, :], w_time.astype(jnp.float32), precision=lax.Precision.HIGHEST
    )[0]


def replicated_gather(piece, name):
    size = lax.axis_size(name)
    copies = jnp.broadcast_to(piece[None], (size,) + piece.shape)
    return lax.all_to_all(copies, name, 0, 0, tiled=True)


def local(
    latent,
    timestep,
    norm_gain,
    norm_bias,
    w_time,
    w_query,
    w_key,
    w_value,
    w_out,
    stale_keys,
    stale_values,
):
    rows_here, chan_width = latent.shape
    chan_count = lax.axis_size("chan")
    device = lax.axis_index(PATCH_AXES)
    local_groups = GROUPS // chan_count
    width = D // GROUPS
    values = latent.astype(jnp.float32).reshape(rows_here, local_groups, width)
    count = rows_here * width
    group_mean = jnp.sum(values, axis=(0, 2)) / count
    spread = jnp.sum(jnp.square(values - group_mean[None, :, None]), axis=(0, 2))
    for name in (PATCH_AXES[1:], PATCH_AXES[0]):
        gathered = replicated_gather(jnp.stack([group_mean, spread]), name)
        group_mean = jnp.mean(gathered[:, 0], axis=0)
        offset = gathered[:, 0] - group_mean[None, :]
        spread = jnp.sum(gathered[:, 1], axis=0) + count * jnp.sum(offset * offset, axis=0)
        count = count * gathered.shape[0]
    variance = spread / count
    centered = values - group_mean[None, :, None]
    scaled = (centered * lax.rsqrt(variance + 1e-05)[None, :, None]).reshape(rows_here, chan_width)
    normed = (scaled * norm_gain + norm_bias + timestep_shift(timestep, w_time)).astype(
        jnp.bfloat16
    )
    inner = w_query.shape[1]
    shard_piece = lax.all_gather(normed, "chan", axis=1, tiled=True)
    outputs = []
    for weight_matrix in (w_query, w_key, w_value):
        outputs.append(jnp.dot(shard_piece, weight_matrix, preferred_element_type=jnp.float32))
    summed = tuple(outputs)
    queries = summed[0].astype(jnp.bfloat16)
    fresh_keys = summed[1].astype(jnp.bfloat16)
    fresh_values = summed[2].astype(jnp.bfloat16)
    heads_here = inner // HEAD_DIM
    score_scale = HEAD_DIM ** (-0.5)
    split = lax.axis_size("px")

    stacked = jnp.stack([stale_keys, stale_values]).reshape(2, rows_here, heads_here, HEAD_DIM)
    stacked = lax.all_to_all(stacked, "px", 2, 1, tiled=True).reshape(2, split * rows_here, HEAD_DIM)
    stacked = jnp.moveaxis(replicated_gather(stacked, "pz"), 0, 1).reshape(2, -1, HEAD_DIM)
    stacked = lax.all_gather(stacked, "py", axis=1, tiled=True)
    slab_count = stacked.shape[1] // rows_here

    fresh = jnp.stack([queries, fresh_keys, fresh_values]).reshape(
        3, rows_here, heads_here, HEAD_DIM
    )
    fresh = lax.all_to_all(fresh, "px", 2, 1, tiled=True)
    fresh = fresh.reshape(3, split, rows_here, HEAD_DIM)
    query_rows = fresh[0].reshape(split * rows_here, HEAD_DIM)

    key_rows = stacked[0]
    value_rows = stacked[1]
    score = (
        jnp.einsum("kd,qd->kq", key_rows, query_rows, preferred_element_type=jnp.float32)
        * score_scale
    ).reshape(slab_count, rows_here, split * rows_here)
    block_max = jnp.max(score, axis=1)
    weight = jnp.exp(score - block_max[:, None, :]).astype(jnp.bfloat16).astype(jnp.float32)

    home_score = (
        jnp.einsum("gqd,gkd->gqk", fresh[0], fresh[1], preferred_element_type=jnp.float32)
        * score_scale
    )
    home_max = jnp.max(home_score, axis=-1)
    home_weight = jnp.exp(home_score - home_max[..., None]).astype(jnp.bfloat16)
    home_num = jnp.einsum("gqk,gkd->gqd", home_weight, fresh[2], preferred_element_type=jnp.float32)
    home_den = jnp.sum(home_weight.astype(jnp.float32), axis=-1)
    home_max = home_max.reshape(split * rows_here)
    home_num = home_num.reshape(split * rows_here, HEAD_DIM)
    home_den = home_den.reshape(split * rows_here)

    first_slab = (device // split) * split
    query_slab = first_slab + jnp.arange(split * rows_here, dtype=jnp.int32) // rows_here
    is_home = jnp.arange(slab_count, dtype=jnp.int32)[:, None] == query_slab[None, :]
    block_max = jnp.where(is_home, home_max[None, :], block_max)
    top = jnp.max(block_max, axis=0)
    factor = jnp.exp(block_max - top[None, :])
    stale_factor = jnp.where(is_home, 0.0, factor)
    scaled_weight = (weight * stale_factor[:, None, :]).reshape(slab_count * rows_here, split * rows_here)
    scaled_weight = scaled_weight.astype(jnp.bfloat16)
    stale_den = jnp.sum(scaled_weight.astype(jnp.float32), axis=0)
    stale_num = jnp.einsum(
        "kd,kq->qd", value_rows, scaled_weight, preferred_element_type=jnp.float32
    )
    home_factor = jnp.exp(home_max - top)
    numer = stale_num + home_factor[:, None] * home_num
    denom = stale_den + home_factor * home_den
    result = (numer / denom[:, None]).astype(jnp.bfloat16)
    result = result.reshape(1, split, rows_here, HEAD_DIM)
    result = jnp.broadcast_to(result, (chan_count, split, rows_here, HEAD_DIM))
    result = result.reshape(chan_count * split, rows_here, HEAD_DIM)
    attended = lax.all_to_all(result, ("chan", "px"), 0, 0, tiled=True)
    attended = jnp.transpose(attended, (1, 0, 2)).reshape(rows_here, chan_count * inner)
    out_columns = lax.all_to_all(w_out, "chan", 1, 0, tiled=True)
    projected = jnp.dot(attended, out_columns, preferred_element_type=jnp.float32)
    mixed = (latent.astype(jnp.float32) + projected).astype(jnp.bfloat16)
    return (mixed, fresh_keys, fresh_values)


def solution(mesh):
    devices = mesh.devices.reshape(PATCH_SPLIT + (mesh.shape["chan"],))
    split_mesh = Mesh(devices, PATCH_AXES + ("chan",))
    rows = PATCH_AXES
    in_specs = (
        P(rows, "chan"),
        P(),
        P("chan"),
        P("chan"),
        P(None, "chan"),
        P(None, "chan"),
        P(None, "chan"),
        P(None, "chan"),
        P("chan", None),
        P(rows, "chan"),
        P(rows, "chan"),
    )
    out_specs = (P(rows, "chan"), P(rows, "chan"), P(rows, "chan"))

    return jax.shard_map(
        local, mesh=split_mesh, in_specs=in_specs, out_specs=out_specs, check_vma=False
    )
```

```python
import math

import jax
import jax.numpy as jnp
from jax import lax
from jax.sharding import Mesh
from jax.sharding import PartitionSpec as P

D = 1280
HEAD_DIM = 64
GROUPS = 32
PATCH_AXES = ("py", "pz", "px")
PATCH_SPLIT = (8, 4, 4)


def timestep_shift(timestep, w_time):
    half_dim = w_time.shape[0] // 2
    frequency = jnp.exp(-math.log(10000.0) * jnp.arange(half_dim, dtype=jnp.float32) / half_dim)
    angles = timestep[0].astype(jnp.float32) * frequency
    embedding = jnp.concatenate([jnp.cos(angles), jnp.sin(angles)])
    return jnp.dot(
        jax.nn.silu(embedding)[None, :], w_time.astype(jnp.float32), precision=lax.Precision.HIGHEST
    )[0]


def patch_sum(partial):
    for name in reversed(PATCH_AXES):
        partial = lax.optimization_barrier(lax.psum(partial, name))
    return partial


def replicated_gather(piece, name):
    size = lax.axis_size(name)
    copies = jnp.broadcast_to(piece[None], (size,) + piece.shape)
    return lax.all_to_all(copies, name, 0, 0, tiled=True)


def permute_gather(piece, name):
    size = lax.axis_size(name)
    here = lax.axis_index(name)
    received = [piece]
    for shift in range(1, size):
        pairs = [(source, (source + shift) % size) for source in range(size)]
        received.append(lax.ppermute(piece, name, pairs))
    received = jnp.stack(received)
    order = (here - jnp.arange(size, dtype=jnp.int32)) % size
    blocks = jnp.take(received, order, axis=0)
    blocks = jnp.moveaxis(blocks, 0, 1)
    return blocks.reshape(piece.shape[0], size * piece.shape[1], *piece.shape[2:])


def local(
    latent,
    timestep,
    norm_gain,
    norm_bias,
    w_time,
    w_query,
    w_key,
    w_value,
    w_out,
    stale_keys,
    stale_values,
):
    rows_here, chan_width = latent.shape
    patch_count = math.prod(lax.axis_size(name) for name in PATCH_AXES)
    chan_count = lax.axis_size("chan")
    device = lax.axis_index(PATCH_AXES)
    local_groups = GROUPS // chan_count
    width = D // GROUPS
    values = latent.astype(jnp.float32).reshape(rows_here, local_groups, width)
    count = rows_here * width
    group_mean = jnp.sum(values, axis=(0, 2)) / count
    spread = jnp.sum(jnp.square(values - group_mean[None, :, None]), axis=(0, 2))
    for name in (PATCH_AXES[1:], PATCH_AXES[0]):
        gathered = replicated_gather(jnp.stack([group_mean, spread]), name)
        group_mean = jnp.mean(gathered[:, 0], axis=0)
        offset = gathered[:, 0] - group_mean[None, :]
        spread = jnp.sum(gathered[:, 1], axis=0) + count * jnp.sum(offset * offset, axis=0)
        count = count * gathered.shape[0]
    variance = spread / count
    centered = values - group_mean[None, :, None]
    scaled = (centered * lax.rsqrt(variance + 1e-05)[None, :, None]).reshape(rows_here, chan_width)
    normed = (scaled * norm_gain + norm_bias + timestep_shift(timestep, w_time)).astype(
        jnp.bfloat16
    )
    inner = w_query.shape[1]
    shard_piece = lax.all_gather(normed, "chan", axis=1, tiled=True)
    outputs = []
    for index, weight_matrix in enumerate((w_query, w_key, w_value)):
        outputs.append(jnp.dot(shard_piece, weight_matrix, preferred_element_type=jnp.float32))
    summed = tuple(outputs)
    queries = summed[0].astype(jnp.bfloat16)
    fresh_keys = summed[1].astype(jnp.bfloat16)
    fresh_values = summed[2].astype(jnp.bfloat16)
    heads_here = inner // HEAD_DIM
    score_scale = HEAD_DIM ** (-0.5)
    split = lax.axis_size("px")
    own_head = lax.axis_index("px")

    stacked = jnp.stack([stale_keys, stale_values]).reshape(2, rows_here, heads_here, HEAD_DIM)
    stacked = lax.all_to_all(stacked, "px", 2, 1, tiled=True).reshape(2, split * rows_here, HEAD_DIM)
    stacked = jnp.moveaxis(replicated_gather(stacked, "pz"), 0, 1).reshape(2, -1, HEAD_DIM)
    stacked = lax.all_gather(stacked, "py", axis=1, tiled=True)
    slab_count = stacked.shape[1] // rows_here

    fresh = jnp.stack([queries, fresh_keys, fresh_values]).reshape(
        3, rows_here, heads_here, HEAD_DIM
    )
    fresh = lax.all_to_all(fresh, "px", 2, 1, tiled=True).reshape(3, split, rows_here, HEAD_DIM)
    query_rows = fresh[0].reshape(split * rows_here, HEAD_DIM)

    key_rows = stacked[0]
    value_rows = stacked[1]
    score = (
        jnp.einsum("kd,qd->kq", key_rows, query_rows, preferred_element_type=jnp.float32)
        * score_scale
    ).reshape(slab_count, rows_here, split * rows_here)
    block_max = jnp.max(score, axis=1)
    weight = jnp.exp(score - block_max[:, None, :]).astype(jnp.bfloat16).astype(jnp.float32)

    home_score = (
        jnp.einsum("gqd,gkd->gqk", fresh[0], fresh[1], preferred_element_type=jnp.float32)
        * score_scale
    )
    home_max = jnp.max(home_score, axis=-1)
    home_weight = jnp.exp(home_score - home_max[..., None]).astype(jnp.bfloat16)
    home_num = jnp.einsum("gqk,gkd->gqd", home_weight, fresh[2], preferred_element_type=jnp.float32)
    home_den = jnp.sum(home_weight.astype(jnp.float32), axis=-1)
    home_max = home_max.reshape(split * rows_here)
    home_num = home_num.reshape(split * rows_here, HEAD_DIM)
    home_den = home_den.reshape(split * rows_here)

    first_slab = (device // split) * split
    query_slab = first_slab + jnp.arange(split * rows_here, dtype=jnp.int32) // rows_here
    is_home = jnp.arange(slab_count, dtype=jnp.int32)[:, None] == query_slab[None, :]
    block_max = jnp.where(is_home, home_max[None, :], block_max)
    top = jnp.max(block_max, axis=0)
    factor = jnp.exp(block_max - top[None, :])
    stale_factor = jnp.where(is_home, 0.0, factor)
    scaled_weight = (weight * stale_factor[:, None, :]).reshape(slab_count * rows_here, split * rows_here)
    scaled_weight = scaled_weight.astype(jnp.bfloat16)
    stale_den = jnp.sum(scaled_weight.astype(jnp.float32), axis=0)
    stale_num = jnp.einsum(
        "kd,kq->qd", value_rows, scaled_weight, preferred_element_type=jnp.float32
    )
    home_factor = jnp.exp(home_max - top)
    numer = stale_num + home_factor[:, None] * home_num
    denom = stale_den + home_factor * home_den
    result = (numer / denom[:, None]).astype(jnp.bfloat16)
    result = result.reshape(split, rows_here, 1, HEAD_DIM)
    attended = lax.all_to_all(result, "px", 0, 2, tiled=True).reshape(rows_here, inner)
    partial = jnp.dot(attended, w_out, preferred_element_type=jnp.float32)
    partial = jnp.moveaxis(partial.reshape(rows_here, chan_count, chan_width), 1, 0)
    projected = jnp.sum(lax.all_to_all(partial, "chan", 0, 0, tiled=True), axis=0)
    mixed = (latent.astype(jnp.float32) + projected).astype(jnp.bfloat16)
    return (mixed, fresh_keys, fresh_values)


def solution(mesh):
    devices = mesh.devices.reshape(PATCH_SPLIT + (mesh.shape["chan"],))
    split_mesh = Mesh(devices, PATCH_AXES + ("chan",))
    rows = PATCH_AXES
    in_specs = (
        P(rows, "chan"),
        P(),
        P("chan"),
        P("chan"),
        P(None, "chan"),
        P(None, "chan"),
        P(None, "chan"),
        P(None, "chan"),
        P("chan", None),
        P(rows, "chan"),
        P(rows, "chan"),
    )
    out_specs = (P(rows, "chan"), P(rows, "chan"), P(rows, "chan"))
    return jax.shard_map(
        local, mesh=split_mesh, in_specs=in_specs, out_specs=out_specs, check_vma=False
    )
```

```python
import math

import jax
import jax.numpy as jnp
from jax import lax
from jax.sharding import Mesh
from jax.sharding import PartitionSpec as P

D = 1280
HEAD_DIM = 64
GROUPS = 32
PATCH_AXES = ("py", "pz", "px")
PATCH_SPLIT = (8, 4, 4)


def timestep_shift(timestep, w_time):
    half_dim = w_time.shape[0] // 2
    frequency = jnp.exp(-math.log(10000.0) * jnp.arange(half_dim, dtype=jnp.float32) / half_dim)
    angles = timestep[0].astype(jnp.float32) * frequency
    embedding = jnp.concatenate([jnp.cos(angles), jnp.sin(angles)])
    return jnp.dot(
        jax.nn.silu(embedding)[None, :], w_time.astype(jnp.float32), precision=lax.Precision.HIGHEST
    )[0]


def patch_sum(partial):
    for name in reversed(PATCH_AXES):
        partial = lax.optimization_barrier(lax.psum(partial, name))
    return partial


def replicated_gather(piece, name):
    size = lax.axis_size(name)
    copies = jnp.broadcast_to(piece[None], (size,) + piece.shape)
    return lax.all_to_all(copies, name, 0, 0, tiled=True)


def permute_gather(piece, name):
    size = lax.axis_size(name)
    here = lax.axis_index(name)
    received = [piece]
    for shift in range(1, size):
        pairs = [(source, (source + shift) % size) for source in range(size)]
        received.append(lax.ppermute(piece, name, pairs))
    received = jnp.stack(received)
    order = (here - jnp.arange(size, dtype=jnp.int32)) % size
    blocks = jnp.take(received, order, axis=0)
    blocks = jnp.moveaxis(blocks, 0, 1)
    return blocks.reshape(piece.shape[0], size * piece.shape[1], *piece.shape[2:])


def local(
    latent,
    timestep,
    norm_gain,
    norm_bias,
    w_time,
    w_query,
    w_key,
    w_value,
    w_out,
    stale_keys,
    stale_values,
):
    rows_here, chan_width = latent.shape
    patch_count = math.prod(lax.axis_size(name) for name in PATCH_AXES)
    chan_count = lax.axis_size("chan")
    device = lax.axis_index(PATCH_AXES)
    local_groups = GROUPS // chan_count
    width = D // GROUPS
    values = latent.astype(jnp.float32).reshape(rows_here, local_groups, width)
    count = rows_here * width
    group_mean = jnp.sum(values, axis=(0, 2)) / count
    spread = jnp.sum(jnp.square(values - group_mean[None, :, None]), axis=(0, 2))
    for name in (PATCH_AXES[0], PATCH_AXES[1:]):
        gathered = replicated_gather(jnp.stack([group_mean, spread]), name)
        group_mean = jnp.mean(gathered[:, 0], axis=0)
        offset = gathered[:, 0] - group_mean[None, :]
        spread = jnp.sum(gathered[:, 1], axis=0) + count * jnp.sum(offset * offset, axis=0)
        count = count * gathered.shape[0]
    variance = spread / count
    centered = values - group_mean[None, :, None]
    scaled = (centered * lax.rsqrt(variance + 1e-05)[None, :, None]).reshape(rows_here, chan_width)
    normed = (scaled * norm_gain + norm_bias + timestep_shift(timestep, w_time)).astype(
        jnp.bfloat16
    )
    inner = w_query.shape[1]
    shard_piece = lax.all_gather(normed, "chan", axis=1, tiled=True)
    outputs = []
    for index, weight_matrix in enumerate((w_query, w_key, w_value)):
        outputs.append(jnp.dot(shard_piece, weight_matrix, preferred_element_type=jnp.float32))
    summed = tuple(outputs)
    queries = summed[0].astype(jnp.bfloat16)
    fresh_keys = summed[1].astype(jnp.bfloat16)
    fresh_values = summed[2].astype(jnp.bfloat16)
    heads_here = inner // HEAD_DIM
    score_scale = HEAD_DIM ** (-0.5)
    split = lax.axis_size("px")
    own_head = lax.axis_index("px")

    stacked = jnp.stack([stale_keys, stale_values]).reshape(2, rows_here, heads_here, HEAD_DIM)
    stacked = lax.all_to_all(stacked, "px", 2, 1, tiled=True).reshape(2, split * rows_here, HEAD_DIM)
    stacked = jnp.moveaxis(replicated_gather(stacked, "pz"), 0, 1).reshape(2, -1, HEAD_DIM)
    stacked = lax.all_gather(stacked, "py", axis=1, tiled=True)
    slab_count = stacked.shape[1] // rows_here

    fresh = jnp.stack([queries, fresh_keys, fresh_values]).reshape(
        3, rows_here, heads_here, HEAD_DIM
    )
    fresh = lax.all_to_all(fresh, "px", 2, 1, tiled=True).reshape(3, split, rows_here, HEAD_DIM)
    query_rows = fresh[0].reshape(split * rows_here, HEAD_DIM)

    key_rows = stacked[0]
    value_rows = stacked[1]
    score = (
        jnp.einsum("kd,qd->kq", key_rows, query_rows, preferred_element_type=jnp.float32)
        * score_scale
    ).reshape(slab_count, rows_here, split * rows_here)
    block_max = jnp.max(score, axis=1)
    weight = jnp.exp(score - block_max[:, None, :]).astype(jnp.bfloat16).astype(jnp.float32)

    home_score = (
        jnp.einsum("gqd,gkd->gqk", fresh[0], fresh[1], preferred_element_type=jnp.float32)
        * score_scale
    )
    home_max = jnp.max(home_score, axis=-1)
    home_weight = jnp.exp(home_score - home_max[..., None]).astype(jnp.bfloat16)
    home_num = jnp.einsum("gqk,gkd->gqd", home_weight, fresh[2], preferred_element_type=jnp.float32)
    home_den = jnp.sum(home_weight.astype(jnp.float32), axis=-1)
    home_max = home_max.reshape(split * rows_here)
    home_num = home_num.reshape(split * rows_here, HEAD_DIM)
    home_den = home_den.reshape(split * rows_here)

    first_slab = (device // split) * split
    query_slab = first_slab + jnp.arange(split * rows_here, dtype=jnp.int32) // rows_here
    is_home = jnp.arange(slab_count, dtype=jnp.int32)[:, None] == query_slab[None, :]
    block_max = jnp.where(is_home, home_max[None, :], block_max)
    top = jnp.max(block_max, axis=0)
    factor = jnp.exp(block_max - top[None, :])
    stale_factor = jnp.where(is_home, 0.0, factor)
    scaled_weight = (weight * stale_factor[:, None, :]).reshape(slab_count * rows_here, split * rows_here)
    scaled_weight = scaled_weight.astype(jnp.bfloat16)
    stale_den = jnp.sum(scaled_weight.astype(jnp.float32), axis=0)
    stale_num = jnp.einsum(
        "kd,kq->qd", value_rows, scaled_weight, preferred_element_type=jnp.float32
    )
    home_factor = jnp.exp(home_max - top)
    numer = stale_num + home_factor[:, None] * home_num
    denom = stale_den + home_factor * home_den
    result = (numer / denom[:, None]).astype(jnp.bfloat16)
    result = result.reshape(split, rows_here, 1, HEAD_DIM)
    attended = lax.all_to_all(result, "px", 0, 2, tiled=True).reshape(rows_here, inner)
    partial = jnp.dot(attended, w_out, preferred_element_type=jnp.float32)
    partial = jnp.moveaxis(partial.reshape(rows_here, chan_count, chan_width), 1, 0)
    projected = jnp.sum(lax.all_to_all(partial, "chan", 0, 0, tiled=True), axis=0)
    mixed = (latent.astype(jnp.float32) + projected).astype(jnp.bfloat16)
    return (mixed, fresh_keys, fresh_values)


def solution(mesh):
    devices = mesh.devices.reshape(PATCH_SPLIT + (mesh.shape["chan"],))
    split_mesh = Mesh(devices, PATCH_AXES + ("chan",))
    rows = PATCH_AXES
    in_specs = (
        P(rows, "chan"),
        P(),
        P("chan"),
        P("chan"),
        P(None, "chan"),
        P(None, "chan"),
        P(None, "chan"),
        P(None, "chan"),
        P("chan", None),
        P(rows, "chan"),
        P(rows, "chan"),
    )
    out_specs = (P(rows, "chan"), P(rows, "chan"), P(rows, "chan"))
    return jax.shard_map(
        local, mesh=split_mesh, in_specs=in_specs, out_specs=out_specs, check_vma=False
    )
```
